512 devices in a mesh: section: 32 (over z_lo, y, core), seq: 16 (over x, z_hi).
Axes of the slice: x: 4, y: 4, z: 16 (z_hi: 4, z_lo: 4; z = z_hi * 4 + z_lo), core: 2. Of those that a mesh axis runs over, the one named last changes fastest.
Arguments:
- up_activation: bfloat16 [32, 2048, 4096], P('section', 'seq'), as said below
- saved_projections: bfloat16 [32, 2048, 768], P('section', 'seq'), as said below
- up_cotangent: bfloat16 [32, 2048, 4096], P('section', 'seq'), may hold values from -6 to 6
- up_input_weight: bfloat16 [32, 4096, 768], P('section', 'seq'), may hold values from -0.09375 to 0.09375
- up_output_weight: bfloat16 [32, 512, 4096], P('section', None, 'seq'), may hold values from -0.25 to 0.25
- upward_gain: float32 [32, 4096], P('section'), may hold values from 0.5 to 1.5
- accum_input: bfloat16 [32, 4096, 768], P('section', 'seq'), may hold values from -48 to 48
- doc_starts: int32 [32, 2048], P('section', 'seq'), may hold values from 0 to 2047, as said below
Outputs:
- upward_grad: bfloat16 [32, 2048, 4096], P('section', 'seq')
- project_grads: bfloat16 [32, 4096, 768], P('section', 'seq')
The draws below stay inside these ranges and needn't reach their ends.
Inputs may be any that keep to these rules, and one draw needn't show every extreme that they name: doc_starts[s, t] is the position of the first token of the document holding token t: it is 0 at t = 0, equals t or doc_starts[s, t - 1] elsewhere, and the last token of every micro-batch starts a document. `up_activation`: saved inputs of the upward layers. `saved_projections`: saved queries, keys and values of the upward layers.
All inputs are finite; a program needn't handle non-finite values.
Results may differ from the reference program's by a relative error of at most 0.014.
Values may be sent and summed in bfloat16 or wider, within the bound.
No kernel may reach another device: no remote copies, remote signals or barrier semaphores. Data moves between devices by JAX's collectives and lax.ppermute only.
A program may use at most 64 MiB of HBM per device.

```python
import jax
import jax.numpy as jnp
from jax import lax

D = 4096
HEAD = 128
GROUP = 4
SECTIONS = 32
SEQ = 2048


def normal_clip(key, shape):
    return jnp.clip(jax.random.normal(key, shape, jnp.float32), -5.0, 5.0)


def draw_up_activation(key, part):
    parts = jax.random.split(jax.random.fold_in(key, 12), 1)
    base = normal_clip(parts[0], (SECTIONS, SEQ, D))
    return base.astype(jnp.bfloat16)


def draw_saved_projections(key, part):
    parts = jax.random.split(jax.random.fold_in(key, 13), 3)
    query = normal_clip(parts[0], (SECTIONS, SEQ, GROUP * HEAD))
    keys = normal_clip(parts[1], (SECTIONS, SEQ, HEAD))
    values = normal_clip(parts[2], (SECTIONS, SEQ, HEAD))
    return jnp.concatenate([query, keys, values], axis=-1).astype(jnp.bfloat16)


def draw_doc_starts(key, part):
    coins = jax.random.randint(jax.random.fold_in(key, 15), (SECTIONS, SEQ), 0, SEQ)
    places = jnp.arange(SEQ, dtype=jnp.int32)
    flags = (coins < 3) | (places == 0)[None, :] | (places == SEQ - 1)[None, :]
    marks = jnp.where(flags, places[None, :], 0).astype(jnp.int32)
    return lax.cummax(marks, axis=1).astype(jnp.int32)


def steps_of(own_key, extent, cuts, smallest, high):
    loudness, own = 1.0, jax.random.fold_in(own_key, 6)
    for axis_at, blocks in cuts:
        draws = jnp.exp(jax.random.uniform(jax.random.fold_in(own, axis_at), (blocks,), jnp.float32, smallest / len(cuts), high / len(cuts)))
        loudness = loudness * jnp.repeat(draws, extent[axis_at] // blocks).reshape([-1 if axis == axis_at else 1 for axis in range(len(extent))])
    return loudness


def normal_values(rng, dims, spread, bound, shards=(), held_as=jnp.bfloat16):
    result = spread * jax.random.normal(rng, dims, jnp.float32)
    if shards:
        result = result * steps_of(rng, dims, shards, -0.22, 0.18)
    return jnp.clip(result, -bound, bound).astype(held_as)


def setup_inputs(seed: int = 0) -> dict:
    streams_of = jax.random.split(jax.random.key(seed), 9)
    up_activation = draw_up_activation(jax.random.fold_in(streams_of[8], 71), 0)
    saved_projections = draw_saved_projections(jax.random.fold_in(streams_of[8], 71), 0)
    up_cotangent = normal_values(streams_of[2], (SECTIONS, SEQ, D), 1.0, 6.0, ((0, 32), (1, 16)))
    up_input_weight = normal_values(streams_of[3], (SECTIONS, D, (GROUP + 2) * HEAD), D ** -0.5, 0.09375, ((0, 32), (1, 16)))
    up_output_weight = normal_values(streams_of[4], (SECTIONS, GROUP * HEAD, D), (GROUP * HEAD) ** -0.5, 0.25, ((0, 32), (2, 16)))
    upward_gain = jnp.clip(1.0 + 0.1 * jax.random.normal(streams_of[5], (SECTIONS, D), jnp.float32), 0.5, 1.5)
    accum_input = normal_values(streams_of[6], (SECTIONS, D, (GROUP + 2) * HEAD), 8.0, 48.0, ((0, 32), (1, 16)))
    doc_starts = draw_doc_starts(jax.random.fold_in(streams_of[8], 71), 0)
    return dict(up_activation=up_activation, saved_projections=saved_projections, up_cotangent=up_cotangent, up_input_weight=up_input_weight, up_output_weight=up_output_weight, upward_gain=upward_gain, accum_input=accum_input, doc_starts=doc_starts)


def normalize(values, gain):
    floats = values.astype(jnp.float32)
    inverse = lax.rsqrt(lax.optimization_barrier(jnp.mean(floats * floats, axis=-1, keepdims=True)) + 1e-05)
    unit = floats * inverse
    return (unit, inverse, unit * gain)

def backward_layer(items):
    rows, saved, cotangent, input_weight, output_weight, gain, starts = items
    width = GROUP * HEAD
    unit, inverse, normed = normalize(rows, gain)
    hidden = normed.astype(jnp.bfloat16)
    query = saved[:, :width].reshape(SEQ, GROUP, HEAD).astype(jnp.float32)
    keys = saved[:, width:width + HEAD].astype(jnp.float32)
    values = saved[:, width + HEAD:].astype(jnp.float32)
    positions = jnp.arange(SEQ, dtype=jnp.int32)
    visible = (positions[None, :] <= positions[:, None]) & (positions[None, :] >= starts[:, None])
    scores = jnp.einsum('tgh,jh->tgj', query, keys) * HEAD ** (-0.5)
    scores = jnp.where(visible[:, None, :], scores, -1e+30)
    top = lax.optimization_barrier(jnp.max(scores, axis=-1, keepdims=True))
    exps = jnp.where(visible[:, None, :], jnp.exp(scores - top), 0.0)
    probs = exps / lax.optimization_barrier(jnp.sum(exps, axis=-1, keepdims=True))
    weights = probs.astype(jnp.bfloat16)
    attn_grad = jnp.dot(cotangent, output_weight.T, preferred_element_type=jnp.float32).astype(jnp.bfloat16)
    grad_heads = attn_grad.reshape(SEQ, GROUP, HEAD).astype(jnp.float32)
    prob_grad = jnp.einsum('tgh,jh->tgj', grad_heads, values)
    inner = lax.optimization_barrier(jnp.sum(probs * prob_grad, axis=-1, keepdims=True))
    score_grad = (probs * (prob_grad - inner) * HEAD ** (-0.5)).astype(jnp.bfloat16)
    score_float = score_grad.astype(jnp.float32)
    query_grad = jnp.einsum('tgj,jh->tgh', score_float, keys).astype(jnp.bfloat16).reshape(SEQ, width)
    key_grad = jnp.einsum('tgj,tgh->jh', score_float, query).astype(jnp.bfloat16)
    value_grad = jnp.einsum('tgj,tgh->jh', weights.astype(jnp.float32), grad_heads).astype(jnp.bfloat16)
    proj_grad = jnp.concatenate([query_grad, key_grad, value_grad], axis=1)
    input_term = jnp.dot(hidden.T, proj_grad, preferred_element_type=jnp.float32).astype(jnp.bfloat16)
    hidden_grad = jnp.dot(proj_grad, input_weight.T, preferred_element_type=jnp.float32)
    scaled = hidden_grad * gain
    input_grad = cotangent.astype(jnp.float32) + inverse * (scaled - unit * lax.optimization_barrier(jnp.mean(scaled * unit, axis=-1, keepdims=True)))
    return (input_grad.astype(jnp.bfloat16), input_term)

def reference(up_activation, saved_projections, up_cotangent, up_input_weight, up_output_weight, upward_gain, accum_input, doc_starts):
    input_grad, input_term = lax.map(backward_layer, (up_activation, saved_projections, up_cotangent, up_input_weight, up_output_weight, upward_gain, doc_starts))
    upward_grad = jnp.concatenate([jnp.zeros_like(input_grad[:1]), input_grad[:-1]], axis=0)
    project_grads = (accum_input.astype(jnp.float32) + input_term[::-1].astype(jnp.float32)).astype(jnp.bfloat16)
    return (upward_grad, project_grads)
```

```python
import jax
import jax.numpy as jnp
from jax import lax
from jax.sharding import PartitionSpec as P

HEAD = 128
GROUP = 4
INNER = 4


def shifted(value, axis, steps):
    count = lax.axis_size(axis)
    initial, last = (max(0, -steps), min(count, count - steps))
    return lax.ppermute(value, axis, [(source, source + steps) for source in range(initial, last)])


def mirrored(value, axis):
    count = lax.axis_size(axis)
    return lax.ppermute(value, axis, [(source, count - 1 - source) for source in range(count)])


def seq_pairs(shift, level):
    size = lax.axis_size("seq")
    outer = size // INNER
    if level == 0:
        return [(o * INNER + i, o * INNER + (i + shift) % INNER) for o in range(outer) for i in range(INNER)]
    return [(o * INNER + i, ((o + shift) % outer) * INNER + i) for o in range(outer) for i in range(INNER)]


def gather_blocks(x):
    outer = lax.axis_size("seq") // INNER
    first = jnp.stack([x] + [lax.ppermute(x, "seq", seq_pairs(k, 0)) for k in range(1, INNER)])
    return jnp.stack([first] + [lax.ppermute(first, "seq", seq_pairs(k, 1)) for k in range(1, outer)])


def reduce_blocks(y):
    outer = lax.axis_size("seq") // INNER
    acc = y[0]
    for k in range(1, outer):
        acc = acc + lax.ppermute(y[k], "seq", seq_pairs(outer - k, 1))
    total = acc[0]
    for k in range(1, INNER):
        total = total + lax.ppermute(acc[k], "seq", seq_pairs(INNER - k, 0))
    return total


def scatter_columns(x, o, i):
    outer = lax.axis_size("seq") // INNER
    n = x.shape[0]
    parts = x.reshape(n, outer, INNER, -1).transpose(2, 1, 0, 3)
    first = [parts[i]]
    for k in range(1, INNER):
        piece = lax.dynamic_index_in_dim(parts, (i + k) % INNER, 0, keepdims=False)
        first.append(lax.ppermute(piece, "seq", seq_pairs(k, 0)))
    first = jnp.stack(first, axis=1)
    second = [first[o]]
    for k in range(1, outer):
        piece = lax.dynamic_index_in_dim(first, (o + k) % outer, 0, keepdims=False)
        second.append(lax.ppermute(piece, "seq", seq_pairs(k, 1)))
    return jnp.stack(second)


def gather_columns(y, o, i):
    outer = lax.axis_size("seq") // INNER
    n, w = y.shape[2], y.shape[3]
    first = [y[0]]
    for k in range(1, outer):
        first.append(lax.ppermute(y[k], "seq", seq_pairs(outer - k, 1)))
    first = jnp.stack(first, axis=1)
    second = [first[0]]
    for k in range(1, INNER):
        second.append(lax.ppermute(first[k], "seq", seq_pairs(INNER - k, 0)))
    second = jnp.stack(second, axis=1)
    second = jnp.roll(jnp.roll(second, o, axis=0), i, axis=1)
    return second.transpose(2, 0, 1, 3).reshape(n, outer * INNER * w)


def contract_last(left, right):
    return lax.dot_general(
        left, right, (((1,), (1,)), ((), ())), preferred_element_type=jnp.float32
    )


def contract_first(left, right):
    return lax.dot_general(
        left, right, (((0,), (0,)), ((), ())), preferred_element_type=jnp.float32
    )


def normalize(values, gain):
    floats = values.astype(jnp.float32)
    inverse = lax.rsqrt(jnp.mean(floats * floats, axis=-1, keepdims=True) + 1e-05)
    unit = floats * inverse
    return (unit, inverse, unit * gain)


def per_device(
    up_activation,
    saved_projections,
    up_cotangent,
    up_input_weight,
    up_output_weight,
    upward_gain,
    accum_input,
    doc_starts,
):
    factor = HEAD ** (-0.5)
    width = GROUP * HEAD
    count = up_activation.shape[1]
    size = lax.axis_size("seq")
    outer = size // INNER
    me = lax.axis_index("seq")
    o, i = me // INNER, me % INNER
    first = me * count
    saved = saved_projections[0]
    cotangent = up_cotangent[0]
    unit_up, inverse_up, normed_up = normalize(up_activation[0], upward_gain[0])
    hidden = normed_up.astype(jnp.bfloat16)
    output_weight = lax.all_gather(up_output_weight[0], "seq", axis=1, tiled=True)
    key_value = gather_blocks(saved[:, width:]).reshape(size * count, 2 * HEAD)
    keys = key_value[:, :HEAD]
    values = key_value[:, HEAD:]
    sources = (
        ((o - jnp.arange(outer, dtype=jnp.int32)) % outer)[:, None] * INNER
        + ((i - jnp.arange(INNER, dtype=jnp.int32)) % INNER)[None, :]
    ).reshape(size)
    key_positions = (sources[:, None] * count + jnp.arange(count, dtype=jnp.int32)[None, :]).reshape(-1)
    hidden_cols = scatter_columns(hidden, o, i).reshape(size * count, -1)
    query = saved[:, :width].reshape(count, GROUP, HEAD)
    attn_grad = contract_last(cotangent, output_weight).astype(jnp.bfloat16)
    positions = first + jnp.arange(count, dtype=jnp.int32)
    starts = doc_starts[0]
    visible = (key_positions[None, :] <= positions[:, None]) & (
        key_positions[None, :] >= starts[:, None]
    )
    scores = jnp.einsum("tgh,jh->tgj", query, keys, preferred_element_type=jnp.float32) * factor
    scores = jnp.where(visible[:, None, :], scores, -1e30)
    top = jnp.max(scores, axis=-1, keepdims=True)
    exps = jnp.where(visible[:, None, :], jnp.exp(scores - top), 0.0)
    probs = exps / jnp.sum(exps, axis=-1, keepdims=True)
    weights = probs.astype(jnp.bfloat16)
    grad_heads = attn_grad.reshape(count, GROUP, HEAD)
    prob_grad = jnp.einsum("tgh,jh->tgj", grad_heads, values, preferred_element_type=jnp.float32)
    inner = jnp.sum(probs * prob_grad, axis=-1, keepdims=True)
    score_grad = (probs * (prob_grad - inner) * factor).astype(jnp.bfloat16)
    query_grad = (
        jnp.einsum("tgj,jh->tgh", score_grad, keys, preferred_element_type=jnp.float32)
        .astype(jnp.bfloat16)
        .reshape(count, width)
    )
    key_part = jnp.einsum("tgj,tgh->jh", score_grad, query, preferred_element_type=jnp.float32)
    value_part = jnp.einsum("tgj,tgh->jh", weights, grad_heads, preferred_element_type=jnp.float32)
    kv_part = jnp.concatenate([key_part, value_part], axis=1).reshape(outer, INNER, count, 2 * HEAD)
    kv_grad = reduce_blocks(kv_part).astype(jnp.bfloat16)
    own_grad = jnp.concatenate([query_grad, kv_grad], axis=1)
    grad_all = gather_blocks(own_grad).reshape(size * count, -1)
    input_term = contract_first(hidden_cols, grad_all).astype(jnp.bfloat16)
    block = contract_last(grad_all, up_input_weight[0])
    hidden_grad = gather_columns(block.reshape(outer, INNER, count, -1), o, i)
    scaled = hidden_grad * upward_gain[0]
    input_grad = cotangent.astype(jnp.float32) + inverse_up * (
        scaled - unit_up * jnp.mean(scaled * unit_up, axis=-1, keepdims=True)
    )
    moved_grad = shifted(input_grad.astype(jnp.bfloat16), "section", 1)
    mirror_input = mirrored(input_term, "section")
    project_grads = (accum_input[0].astype(jnp.float32) + mirror_input.astype(jnp.float32)).astype(
        jnp.bfloat16
    )
    return (moved_grad[None], project_grads[None])


def solution(mesh):
    return jax.shard_map(
        per_device,
        mesh=mesh,
        in_specs=(
            P("section", "seq", None),
            P("section", "seq", None),
            P("section", "seq", None),
            P("section", "seq", None),
            P("section", None, "seq"),
            P("section", None),
            P("section", "seq", None),
            P("section", "seq"),
        ),
        out_specs=(P("section", "seq", None), P("section", "seq", None)),
        check_vma=False,
    )
```

```python
import jax
import jax.numpy as jnp
from jax import lax
from jax.sharding import PartitionSpec as P

HEAD = 128
GROUP = 4
INNER = 4


def shifted(value, axis, steps):
    count = lax.axis_size(axis)
    initial, last = (max(0, -steps), min(count, count - steps))
    return lax.ppermute(value, axis, [(source, source + steps) for source in range(initial, last)])


def mirrored(value, axis):
    count = lax.axis_size(axis)
    return lax.ppermute(value, axis, [(source, count - 1 - source) for source in range(count)])


def seq_pairs(shift, level):
    size = lax.axis_size("seq")
    outer = size // INNER
    if level == 0:
        return [(o * INNER + i, o * INNER + (i + shift) % INNER) for o in range(outer) for i in range(INNER)]
    return [(o * INNER + i, ((o + shift) % outer) * INNER + i) for o in range(outer) for i in range(INNER)]


def gather_blocks(x):
    outer = lax.axis_size("seq") // INNER
    first = jnp.stack([x] + [lax.ppermute(x, "seq", seq_pairs(k, 0)) for k in range(1, INNER)])
    return jnp.stack([first] + [lax.ppermute(first, "seq", seq_pairs(k, 1)) for k in range(1, outer)])


def reduce_blocks(y):
    outer = lax.axis_size("seq") // INNER
    acc = y[0]
    for k in range(1, outer):
        acc = acc + lax.ppermute(y[k], "seq", seq_pairs(outer - k, 1))
    total = acc[0]
    for k in range(1, INNER):
        total = total + lax.ppermute(acc[k], "seq", seq_pairs(INNER - k, 0))
    return total


def gather_and_scatter(x, cols, o, i):
    outer = lax.axis_size("seq") // INNER
    n = x.shape[0]
    parts = cols.reshape(n, outer, INNER, -1).transpose(2, 1, 0, 3)
    first = [jnp.concatenate([x[None], parts[i]])]
    for k in range(1, INNER):
        piece = lax.dynamic_index_in_dim(parts, (i + k) % INNER, 0, keepdims=False)
        first.append(lax.ppermute(jnp.concatenate([x[None], piece]), "seq", seq_pairs(k, 0)))
    first = jnp.stack(first, axis=1)
    second = [first]
    for k in range(1, outer):
        piece = lax.dynamic_index_in_dim(first[1:], (o + k) % outer, 0, keepdims=False)
        second.append(lax.ppermute(jnp.concatenate([first[0], piece]), "seq", seq_pairs(k, 1)))
    gathered = jnp.stack([second[0][0]] + [s[:INNER] for s in second[1:]])
    scattered = jnp.stack([second[0][1 + o]] + [s[INNER:] for s in second[1:]])
    return gathered, scattered


def reduce_and_gather(partial, own):
    outer = lax.axis_size("seq") // INNER
    n, w = partial.shape[2], partial.shape[3]
    acc = partial[0]
    for k in range(1, outer):
        acc = acc + lax.ppermute(partial[k], "seq", seq_pairs(outer - k, 1))
    mine = jnp.concatenate([acc.transpose(1, 0, 2).reshape(n, INNER * w), own.astype(jnp.float32)], axis=1)
    total = acc
    rows = [own.astype(jnp.float32)]
    for k in range(1, INNER):
        got = lax.ppermute(mine, "seq", seq_pairs(k, 0))
        sums = got[:, : INNER * w].reshape(n, INNER, w).transpose(1, 0, 2)
        total = total + jnp.roll(sums, k, axis=0)
        rows.append(got[:, INNER * w :])
    group = jnp.concatenate([jnp.stack(rows), total], axis=2).astype(own.dtype)
    return jnp.stack([group] + [lax.ppermute(group, "seq", seq_pairs(k, 1)) for k in range(1, outer)])


def gather_columns(y, o, i):
    outer = lax.axis_size("seq") // INNER
    n, w = y.shape[2], y.shape[3]
    first = [y[0]]
    for k in range(1, outer):
        first.append(lax.ppermute(y[k], "seq", seq_pairs(outer - k, 1)))
    first = jnp.stack(first, axis=1)
    second = [first[0]]
    for k in range(1, INNER):
        second.append(lax.ppermute(first[k], "seq", seq_pairs(INNER - k, 0)))
    second = jnp.stack(second, axis=1)
    second = jnp.roll(jnp.roll(second, o, axis=0), i, axis=1)
    return second.transpose(2, 0, 1, 3).reshape(n, outer * INNER * w)


def contract_last(left, right):
    return lax.dot_general(
        left, right, (((1,), (1,)), ((), ())), preferred_element_type=jnp.float32
    )


def contract_first(left, right):
    return lax.dot_general(
        left, right, (((0,), (0,)), ((), ())), preferred_element_type=jnp.float32
    )


def normalize(values, gain):
    floats = values.astype(jnp.float32)
    inverse = lax.rsqrt(jnp.mean(floats * floats, axis=-1, keepdims=True) + 1e-05)
    unit = floats * inverse
    return (unit, inverse, unit * gain)


def per_device(
    up_activation,
    saved_projections,
    up_cotangent,
    up_input_weight,
    up_output_weight,
    upward_gain,
    accum_input,
    doc_starts,
):
    factor = HEAD ** (-0.5)
    width = GROUP * HEAD
    count = up_activation.shape[1]
    size = lax.axis_size("seq")
    outer = size // INNER
    me = lax.axis_index("seq")
    o, i = me // INNER, me % INNER
    first = me * count
    saved = saved_projections[0]
    cotangent = up_cotangent[0]
    unit_up, inverse_up, normed_up = normalize(up_activation[0], upward_gain[0])
    hidden = normed_up.astype(jnp.bfloat16)
    output_weight = lax.all_gather(up_output_weight[0], "seq", axis=1, tiled=True)
    key_value, hidden_cols = gather_and_scatter(saved[:, width:], hidden, o, i)
    key_value = key_value.reshape(size * count, 2 * HEAD)
    hidden_cols = hidden_cols.reshape(size * count, -1)
    keys = key_value[:, :HEAD]
    values = key_value[:, HEAD:]
    sources = (
        ((o - jnp.arange(outer, dtype=jnp.int32)) % outer)[:, None] * INNER
        + ((i - jnp.arange(INNER, dtype=jnp.int32)) % INNER)[None, :]
    ).reshape(size)
    key_positions = (sources[:, None] * count + jnp.arange(count, dtype=jnp.int32)[None, :]).reshape(-1)
    query = saved[:, :width].reshape(count, GROUP, HEAD)
    attn_grad = contract_last(cotangent, output_weight).astype(jnp.bfloat16)
    positions = first + jnp.arange(count, dtype=jnp.int32)
    starts = doc_starts[0]
    visible = (key_positions[None, :] <= positions[:, None]) & (
        key_positions[None, :] >= starts[:, None]
    )
    scores = jnp.einsum("tgh,jh->tgj", query, keys, preferred_element_type=jnp.float32) * factor
    scores = jnp.where(visible[:, None, :], scores, -1e30)
    top = jnp.max(scores, axis=-1, keepdims=True)
    exps = jnp.where(visible[:, None, :], jnp.exp(scores - top), 0.0)
    probs = exps / jnp.sum(exps, axis=-1, keepdims=True)
    weights = probs.astype(jnp.bfloat16)
    grad_heads = attn_grad.reshape(count, GROUP, HEAD)
    prob_grad = jnp.einsum("tgh,jh->tgj", grad_heads, values, preferred_element_type=jnp.float32)
    inner = jnp.sum(probs * prob_grad, axis=-1, keepdims=True)
    score_grad = (probs * (prob_grad - inner) * factor).astype(jnp.bfloat16)
    query_grad = (
        jnp.einsum("tgj,jh->tgh", score_grad, keys, preferred_element_type=jnp.float32)
        .astype(jnp.bfloat16)
        .reshape(count, width)
    )
    key_part = jnp.einsum("tgj,tgh->jh", score_grad, query, preferred_element_type=jnp.float32)
    value_part = jnp.einsum("tgj,tgh->jh", weights, grad_heads, preferred_element_type=jnp.float32)
    kv_part = jnp.concatenate([key_part, value_part], axis=1).reshape(outer, INNER, count, 2 * HEAD)
    grad_all = reduce_and_gather(kv_part, query_grad).reshape(size * count, -1)
    input_term = contract_first(hidden_cols, grad_all).astype(jnp.bfloat16)
    block = contract_last(grad_all, up_input_weight[0])
    hidden_grad = gather_columns(block.astype(jnp.bfloat16).reshape(outer, INNER, count, -1), o, i)
    hidden_grad = hidden_grad.astype(jnp.float32)
    scaled = hidden_grad * upward_gain[0]
    input_grad = cotangent.astype(jnp.float32) + inverse_up * (
        scaled - unit_up * jnp.mean(scaled * unit_up, axis=-1, keepdims=True)
    )
    moved_grad = shifted(input_grad.astype(jnp.bfloat16), "section", 1)
    mirror_input = mirrored(input_term, "section")
    project_grads = (accum_input[0].astype(jnp.float32) + mirror_input.astype(jnp.float32)).astype(
        jnp.bfloat16
    )
    return (moved_grad[None], project_grads[None])


def solution(mesh):
    return jax.shard_map(
        per_device,
        mesh=mesh,
        in_specs=(
            P("section", "seq", None),
            P("section", "seq", None),
            P("section", "seq", None),
            P("section", "seq", None),
            P("section", None, "seq"),
            P("section", None),
            P("section", "seq", None),
            P("section", "seq"),
        ),
        out_specs=(P("section", "seq", None), P("section", "seq", None)),
        check_vma=False,
    )
```

```python
import jax
import jax.numpy as jnp
from jax import lax
from jax.sharding import PartitionSpec as P

HEAD = 128
GROUP = 4
INNER = 4


def shifted(value, axis, steps):
    count = lax.axis_size(axis)
    initial, last = (max(0, -steps), min(count, count - steps))
    return lax.ppermute(value, axis, [(source, source + steps) for source in range(initial, last)])


def mirrored(value, axis):
    count = lax.axis_size(axis)
    return lax.ppermute(value, axis, [(source, count - 1 - source) for source in range(count)])


def seq_pairs(shift, level):
    size = lax.axis_size("seq")
    outer = size // INNER
    if level == 0:
        return [(o * INNER + i, o * INNER + (i + shift) % INNER) for o in range(outer) for i in range(INNER)]
    return [(o * INNER + i, ((o + shift) % outer) * INNER + i) for o in range(outer) for i in range(INNER)]


def gather_blocks(x):
    outer = lax.axis_size("seq") // INNER
    first = jnp.stack([x] + [lax.ppermute(x, "seq", seq_pairs(k, 0)) for k in range(1, INNER)])
    return jnp.stack([first] + [lax.ppermute(first, "seq", seq_pairs(k, 1)) for k in range(1, outer)])


def reduce_blocks(y):
    outer = lax.axis_size("seq") // INNER
    acc = y[0]
    for k in range(1, outer):
        acc = acc + lax.ppermute(y[k], "seq", seq_pairs(outer - k, 1))
    total = acc[0]
    for k in range(1, INNER):
        total = total + lax.ppermute(acc[k], "seq", seq_pairs(INNER - k, 0))
    return total


def gather_and_scatter(x, cols, o, i):
    outer = lax.axis_size("seq") // INNER
    n = x.shape[0]
    parts = cols.reshape(n, outer, INNER, -1).transpose(2, 1, 0, 3)
    first = [jnp.concatenate([x[None], parts[i]])]
    for k in range(1, INNER):
        piece = lax.dynamic_index_in_dim(parts, (i + k) % INNER, 0, keepdims=False)
        first.append(lax.ppermute(jnp.concatenate([x[None], piece]), "seq", seq_pairs(k, 0)))
    first = jnp.stack(first, axis=1)
    second = [first]
    for k in range(1, outer):
        piece = lax.dynamic_index_in_dim(first[1:], (o + k) % outer, 0, keepdims=False)
        second.append(lax.ppermute(jnp.concatenate([first[0], piece]), "seq", seq_pairs(k, 1)))
    gathered = jnp.stack([second[0][0]] + [s[:INNER] for s in second[1:]])
    scattered = jnp.stack([second[0][1 + o]] + [s[INNER:] for s in second[1:]])
    return gathered, scattered


def gather_columns(y, o, i):
    outer = lax.axis_size("seq") // INNER
    n, w = y.shape[2], y.shape[3]
    first = [y[0]]
    for k in range(1, outer):
        first.append(lax.ppermute(y[k], "seq", seq_pairs(outer - k, 1)))
    first = jnp.stack(first, axis=1)
    second = [first[0]]
    for k in range(1, INNER):
        second.append(lax.ppermute(first[k], "seq", seq_pairs(INNER - k, 0)))
    second = jnp.stack(second, axis=1)
    second = jnp.roll(jnp.roll(second, o, axis=0), i, axis=1)
    return second.transpose(2, 0, 1, 3).reshape(n, outer * INNER * w)


def contract_last(left, right):
    return lax.dot_general(
        left, right, (((1,), (1,)), ((), ())), preferred_element_type=jnp.float32
    )


def contract_first(left, right):
    return lax.dot_general(
        left, right, (((0,), (0,)), ((), ())), preferred_element_type=jnp.float32
    )


def normalize(values, gain):
    floats = values.astype(jnp.float32)
    inverse = lax.rsqrt(jnp.mean(floats * floats, axis=-1, keepdims=True) + 1e-05)
    unit = floats * inverse
    return (unit, inverse, unit * gain)


def per_device(
    up_activation,
    saved_projections,
    up_cotangent,
    up_input_weight,
    up_output_weight,
    upward_gain,
    accum_input,
    doc_starts,
):
    factor = HEAD ** (-0.5)
    width = GROUP * HEAD
    count = up_activation.shape[1]
    size = lax.axis_size("seq")
    outer = size // INNER
    me = lax.axis_index("seq")
    o, i = me // INNER, me % INNER
    first = me * count
    saved = saved_projections[0]
    cotangent = up_cotangent[0]
    unit_up, inverse_up, normed_up = normalize(up_activation[0], upward_gain[0])
    hidden = normed_up.astype(jnp.bfloat16)
    output_weight = lax.all_gather(up_output_weight[0], "seq", axis=1, tiled=True)
    key_value, hidden_cols = gather_and_scatter(saved[:, width:], hidden, o, i)
    key_value = key_value.reshape(size * count, 2 * HEAD)
    hidden_cols = hidden_cols.reshape(size * count, -1)
    keys = key_value[:, :HEAD]
    values = key_value[:, HEAD:]
    sources = (
        ((o - jnp.arange(outer, dtype=jnp.int32)) % outer)[:, None] * INNER
        + ((i - jnp.arange(INNER, dtype=jnp.int32)) % INNER)[None, :]
    ).reshape(size)
    key_positions = (sources[:, None] * count + jnp.arange(count, dtype=jnp.int32)[None, :]).reshape(-1)
    query = saved[:, :width].reshape(count, GROUP, HEAD)
    attn_grad = contract_last(cotangent, output_weight).astype(jnp.bfloat16)
    positions = first + jnp.arange(count, dtype=jnp.int32)
    starts = doc_starts[0]
    visible = (key_positions[None, :] <= positions[:, None]) & (
        key_positions[None, :] >= starts[:, None]
    )
    scores = jnp.einsum("tgh,jh->tgj", query, keys, preferred_element_type=jnp.float32) * factor
    scores = jnp.where(visible[:, None, :], scores, -1e30)
    top = jnp.max(scores, axis=-1, keepdims=True)
    exps = jnp.where(visible[:, None, :], jnp.exp(scores - top), 0.0)
    probs = exps / jnp.sum(exps, axis=-1, keepdims=True)
    weights = probs.astype(jnp.bfloat16)
    grad_heads = attn_grad.reshape(count, GROUP, HEAD)
    prob_grad = jnp.einsum("tgh,jh->tgj", grad_heads, values, preferred_element_type=jnp.float32)
    inner = jnp.sum(probs * prob_grad, axis=-1, keepdims=True)
    score_grad = (probs * (prob_grad - inner) * factor).astype(jnp.bfloat16)
    query_grad = (
        jnp.einsum("tgj,jh->tgh", score_grad, keys, preferred_element_type=jnp.float32)
        .astype(jnp.bfloat16)
        .reshape(count, width)
    )
    key_part = jnp.einsum("tgj,tgh->jh", score_grad, query, preferred_element_type=jnp.float32)
    value_part = jnp.einsum("tgj,tgh->jh", weights, grad_heads, preferred_element_type=jnp.float32)
    kv_part = jnp.concatenate([key_part, value_part], axis=1).reshape(outer, INNER, count, 2 * HEAD)
    kv_grad = reduce_blocks(kv_part).astype(jnp.bfloat16)
    own_grad = jnp.concatenate([query_grad, kv_grad], axis=1)
    grad_all = gather_blocks(own_grad).reshape(size * count, -1)
    input_term = contract_first(hidden_cols, grad_all).astype(jnp.bfloat16)
    block = contract_last(grad_all, up_input_weight[0])
    hidden_grad = gather_columns(block.astype(jnp.bfloat16).reshape(outer, INNER, count, -1), o, i)
    hidden_grad = hidden_grad.astype(jnp.float32)
    scaled = hidden_grad * upward_gain[0]
    input_grad = cotangent.astype(jnp.float32) + inverse_up * (
        scaled - unit_up * jnp.mean(scaled * unit_up, axis=-1, keepdims=True)
    )
    moved_grad = shifted(input_grad.astype(jnp.bfloat16), "section", 1)
    mirror_input = mirrored(input_term, "section")
    project_grads = (accum_input[0].astype(jnp.float32) + mirror_input.astype(jnp.float32)).astype(
        jnp.bfloat16
    )
    return (moved_grad[None], project_grads[None])


def solution(mesh):
    return jax.shard_map(
        per_device,
        mesh=mesh,
        in_specs=(
            P("section", "seq", None),
            P("section", "seq", None),
            P("section", "seq", None),
            P("section", "seq", None),
            P("section", None, "seq"),
            P("section", None),
            P("section", "seq", None),
            P("section", "seq"),
        ),
        out_specs=(P("section", "seq", None), P("section", "seq", None)),
        check_vma=False,
    )
```

```python
import jax
import jax.numpy as jnp
from jax import lax
from jax.sharding import PartitionSpec as P

HEAD = 128
GROUP = 4
INNER = 4


def shifted(value, axis, steps):
    count = lax.axis_size(axis)
    initial, last = (max(0, -steps), min(count, count - steps))
    return lax.ppermute(value, axis, [(source, source + steps) for source in range(initial, last)])


def mirrored(value, axis):
    count = lax.axis_size(axis)
    return lax.ppermute(value, axis, [(source, count - 1 - source) for source in range(count)])


def seq_pairs(shift, level):
    size = lax.axis_size("seq")
    outer = size // INNER
    if level == 0:
        return [(o * INNER + i, o * INNER + (i + shift) % INNER) for o in range(outer) for i in range(INNER)]
    return [(o * INNER + i, ((o + shift) % outer) * INNER + i) for o in range(outer) for i in range(INNER)]


def gather_blocks(x):
    outer = lax.axis_size("seq") // INNER
    first = jnp.stack([x] + [lax.ppermute(x, "seq", seq_pairs(k, 0)) for k in range(1, INNER)])
    return jnp.stack([first] + [lax.ppermute(first, "seq", seq_pairs(k, 1)) for k in range(1, outer)])


def reduce_blocks(y):
    outer = lax.axis_size("seq") // INNER
    acc = y[0]
    for k in range(1, outer):
        acc = acc + lax.ppermute(y[k], "seq", seq_pairs(outer - k, 1))
    total = acc[0]
    for k in range(1, INNER):
        total = total + lax.ppermute(acc[k], "seq", seq_pairs(INNER - k, 0))
    return total


def gather_and_scatter(x, cols, o, i):
    outer = lax.axis_size("seq") // INNER
    n = x.shape[0]
    parts = cols.reshape(n, outer, INNER, -1).transpose(2, 1, 0, 3)
    first = [jnp.concatenate([x[None], parts[i]])]
    for k in range(1, INNER):
        piece = lax.dynamic_index_in_dim(parts, (i + k) % INNER, 0, keepdims=False)
        first.append(lax.ppermute(jnp.concatenate([x[None], piece]), "seq", seq_pairs(k, 0)))
    first = jnp.stack(first, axis=1)
    second = [first]
    for k in range(1, outer):
        piece = lax.dynamic_index_in_dim(first[1:], (o + k) % outer, 0, keepdims=False)
        second.append(lax.ppermute(jnp.concatenate([first[0], piece]), "seq", seq_pairs(k, 1)))
    gathered = jnp.stack([second[0][0]] + [s[:INNER] for s in second[1:]])
    scattered = jnp.stack([second[0][1 + o]] + [s[INNER:] for s in second[1:]])
    return gathered, scattered


def gather_columns(y, o, i):
    outer = lax.axis_size("seq") // INNER
    n, w = y.shape[2], y.shape[3]
    first = [y[0]]
    for k in range(1, outer):
        first.append(lax.ppermute(y[k], "seq", seq_pairs(outer - k, 1)))
    first = jnp.stack(first, axis=1)
    second = [first[0]]
    for k in range(1, INNER):
        second.append(lax.ppermute(first[k], "seq", seq_pairs(INNER - k, 0)))
    second = jnp.stack(second, axis=1)
    second = jnp.roll(jnp.roll(second, o, axis=0), i, axis=1)
    return second.transpose(2, 0, 1, 3).reshape(n, outer * INNER * w)


def contract_last(left, right):
    return lax.dot_general(
        left, right, (((1,), (1,)), ((), ())), preferred_element_type=jnp.float32
    )


def contract_first(left, right):
    return lax.dot_general(
        left, right, (((0,), (0,)), ((), ())), preferred_element_type=jnp.float32
    )


def normalize(values, gain):
    floats = values.astype(jnp.float32)
    inverse = lax.rsqrt(jnp.mean(floats * floats, axis=-1, keepdims=True) + 1e-05)
    unit = floats * inverse
    return (unit, inverse, unit * gain)


def per_device(
    up_activation,
    saved_projections,
    up_cotangent,
    up_input_weight,
    up_output_weight,
    upward_gain,
    accum_input,
    doc_starts,
):
    factor = HEAD ** (-0.5)
    width = GROUP * HEAD
    count = up_activation.shape[1]
    size = lax.axis_size("seq")
    outer = size // INNER
    me = lax.axis_index("seq")
    o, i = me // INNER, me % INNER
    first = me * count
    saved = saved_projections[0]
    cotangent = up_cotangent[0]
    unit_up, inverse_up, normed_up = normalize(up_activation[0], upward_gain[0])
    hidden = normed_up.astype(jnp.bfloat16)
    output_weight = lax.all_gather(up_output_weight[0], "seq", axis=1, tiled=True)
    key_value, hidden_cols = gather_and_scatter(saved[:, width:], hidden, o, i)
    key_value = key_value.reshape(size * count, 2 * HEAD)
    hidden_cols = hidden_cols.reshape(size * count, -1)
    keys = key_value[:, :HEAD]
    values = key_value[:, HEAD:]
    sources = (
        ((o - jnp.arange(outer, dtype=jnp.int32)) % outer)[:, None] * INNER
        + ((i - jnp.arange(INNER, dtype=jnp.int32)) % INNER)[None, :]
    ).reshape(size)
    key_positions = (sources[:, None] * count + jnp.arange(count, dtype=jnp.int32)[None, :]).reshape(-1)
    query = saved[:, :width].reshape(count, GROUP, HEAD)
    attn_grad = contract_last(cotangent, output_weight).astype(jnp.bfloat16)
    positions = first + jnp.arange(count, dtype=jnp.int32)
    starts = doc_starts[0]
    visible = (key_positions[None, :] <= positions[:, None]) & (
        key_positions[None, :] >= starts[:, None]
    )
    scores = jnp.einsum("tgh,jh->tgj", query, keys, preferred_element_type=jnp.float32) * factor
    scores = jnp.where(visible[:, None, :], scores, -1e30)
    top = jnp.max(scores, axis=-1, keepdims=True)
    exps = jnp.where(visible[:, None, :], jnp.exp(scores - top), 0.0)
    probs = exps / jnp.sum(exps, axis=-1, keepdims=True)
    weights = probs.astype(jnp.bfloat16)
    grad_heads = attn_grad.reshape(count, GROUP, HEAD)
    prob_grad = jnp.einsum("tgh,jh->tgj", grad_heads, values, preferred_element_type=jnp.float32)
    inner = jnp.sum(probs * prob_grad, axis=-1, keepdims=True)
    score_grad = (probs * (prob_grad - inner) * factor).astype(jnp.bfloat16)
    query_grad = (
        jnp.einsum("tgj,jh->tgh", score_grad, keys, preferred_element_type=jnp.float32)
        .astype(jnp.bfloat16)
        .reshape(count, width)
    )
    key_part = jnp.einsum("tgj,tgh->jh", score_grad, query, preferred_element_type=jnp.float32)
    value_part = jnp.einsum("tgj,tgh->jh", weights, grad_heads, preferred_element_type=jnp.float32)
    kv_part = jnp.concatenate([key_part, value_part], axis=1).reshape(outer, INNER, count, 2 * HEAD)
    query_all = gather_blocks(query_grad)
    kv_grad = reduce_blocks(kv_part).astype(jnp.bfloat16)
    grad_all = jnp.concatenate([query_all, gather_blocks(kv_grad)], axis=-1).reshape(size * count, -1)
    input_term = contract_first(hidden_cols, grad_all).astype(jnp.bfloat16)
    block = contract_last(grad_all, up_input_weight[0])
    hidden_grad = gather_columns(block.astype(jnp.bfloat16).reshape(outer, INNER, count, -1), o, i)
    hidden_grad = hidden_grad.astype(jnp.float32)
    scaled = hidden_grad * upward_gain[0]
    input_grad = cotangent.astype(jnp.float32) + inverse_up * (
        scaled - unit_up * jnp.mean(scaled * unit_up, axis=-1, keepdims=True)
    )
    moved_grad = shifted(input_grad.astype(jnp.bfloat16), "section", 1)
    mirror_input = mirrored(input_term, "section")
    project_grads = (accum_input[0].astype(jnp.float32) + mirror_input.astype(jnp.float32)).astype(
        jnp.bfloat16
    )
    return (moved_grad[None], project_grads[None])


def solution(mesh):
    return jax.shard_map(
        per_device,
        mesh=mesh,
        in_specs=(
            P("section", "seq", None),
            P("section", "seq", None),
            P("section", "seq", None),
            P("section", "seq", None),
            P("section", None, "seq"),
            P("section", None),
            P("section", "seq", None),
            P("section", "seq"),
        ),
        out_specs=(P("section", "seq", None), P("section", "seq", None)),
        check_vma=False,
    )
```

```python
import jax
import jax.numpy as jnp
from jax import lax
from jax.sharding import PartitionSpec as P

HEAD = 128
GROUP = 4
INNER = 4


def shifted(value, axis, steps):
    count = lax.axis_size(axis)
    initial, last = (max(0, -steps), min(count, count - steps))
    return lax.ppermute(value, axis, [(source, source + steps) for source in range(initial, last)])


def mirrored(value, axis):
    count = lax.axis_size(axis)
    return lax.ppermute(value, axis, [(source, count - 1 - source) for source in range(count)])


def seq_pairs(shift, level):
    size = lax.axis_size("seq")
    outer = size // INNER
    if level == 0:
        return [(o * INNER + i, o * INNER + (i + shift) % INNER) for o in range(outer) for i in range(INNER)]
    return [(o * INNER + i, ((o + shift) % outer) * INNER + i) for o in range(outer) for i in range(INNER)]


def gather_blocks(x):
    outer = lax.axis_size("seq") // INNER
    first = jnp.stack([x] + [lax.ppermute(x, "seq", seq_pairs(k, 0)) for k in range(1, INNER)])
    return jnp.stack([first] + [lax.ppermute(first, "seq", seq_pairs(k, 1)) for k in range(1, outer)])


def reduce_blocks(y):
    outer = lax.axis_size("seq") // INNER
    acc = y[0]
    for k in range(1, outer):
        acc = acc + lax.ppermute(y[k], "seq", seq_pairs(outer - k, 1))
    total = acc[0]
    for k in range(1, INNER):
        total = total + lax.ppermute(acc[k], "seq", seq_pairs(INNER - k, 0))
    return total


def gather_and_scatter(x, cols, o, i):
    outer = lax.axis_size("seq") // INNER
    m, n, w = x.shape
    parts = cols.reshape(n, outer, INNER, w).transpose(2, 1, 0, 3)
    first = [jnp.concatenate([x, parts[i]])]
    for k in range(1, INNER):
        piece = lax.dynamic_index_in_dim(parts, (i + k) % INNER, 0, keepdims=False)
        first.append(lax.ppermute(jnp.concatenate([x, piece]), "seq", seq_pairs(k, 0)))
    first = jnp.stack(first, axis=1)
    own, rest = first[:m], first[m:]
    second = []
    for k in range(1, outer):
        piece = lax.dynamic_index_in_dim(rest, (o + k) % outer, 0, keepdims=False)
        payload = jnp.concatenate([own.reshape(m * INNER, n, w), piece])
        second.append(lax.ppermute(payload, "seq", seq_pairs(k, 1)))
    gathered = jnp.stack([own] + [s[: m * INNER].reshape(m, INNER, n, w) for s in second])
    scattered = jnp.stack([lax.dynamic_index_in_dim(rest, o, 0, keepdims=False)] + [s[m * INNER :] for s in second])
    return gathered, scattered


def gather_columns(y, o, i):
    outer = lax.axis_size("seq") // INNER
    n, w = y.shape[2], y.shape[3]
    first = [y[0]]
    for k in range(1, outer):
        first.append(lax.ppermute(y[k], "seq", seq_pairs(outer - k, 1)))
    first = jnp.stack(first, axis=1)
    second = [first[0]]
    for k in range(1, INNER):
        second.append(lax.ppermute(first[k], "seq", seq_pairs(INNER - k, 0)))
    second = jnp.stack(second, axis=1)
    second = jnp.roll(jnp.roll(second, o, axis=0), i, axis=1)
    return second.transpose(2, 0, 1, 3).reshape(n, outer * INNER * w)


def contract_last(left, right):
    return lax.dot_general(
        left, right, (((1,), (1,)), ((), ())), preferred_element_type=jnp.float32
    )


def contract_first(left, right):
    return lax.dot_general(
        left, right, (((0,), (0,)), ((), ())), preferred_element_type=jnp.float32
    )


def normalize(values, gain):
    floats = values.astype(jnp.float32)
    inverse = lax.rsqrt(jnp.mean(floats * floats, axis=-1, keepdims=True) + 1e-05)
    unit = floats * inverse
    return (unit, inverse, unit * gain)


def per_device(
    up_activation,
    saved_projections,
    up_cotangent,
    up_input_weight,
    up_output_weight,
    upward_gain,
    accum_input,
    doc_starts,
):
    factor = HEAD ** (-0.5)
    width = GROUP * HEAD
    count = up_activation.shape[1]
    size = lax.axis_size("seq")
    outer = size // INNER
    me = lax.axis_index("seq")
    o, i = me // INNER, me % INNER
    first = me * count
    saved = saved_projections[0]
    cotangent = up_cotangent[0]
    unit_up, inverse_up, normed_up = normalize(up_activation[0], upward_gain[0])
    hidden = normed_up.astype(jnp.bfloat16)
    output_weight = lax.all_gather(up_output_weight[0], "seq", axis=1, tiled=True)
    key_value = gather_blocks(saved[:, width:]).reshape(size * count, 2 * HEAD)
    keys = key_value[:, :HEAD]
    values = key_value[:, HEAD:]
    sources = (
        ((o - jnp.arange(outer, dtype=jnp.int32)) % outer)[:, None] * INNER
        + ((i - jnp.arange(INNER, dtype=jnp.int32)) % INNER)[None, :]
    ).reshape(size)
    key_positions = (sources[:, None] * count + jnp.arange(count, dtype=jnp.int32)[None, :]).reshape(-1)
    query = saved[:, :width].reshape(count, GROUP, HEAD)
    attn_grad = contract_last(cotangent, output_weight).astype(jnp.bfloat16)
    positions = first + jnp.arange(count, dtype=jnp.int32)
    starts = doc_starts[0]
    visible = (key_positions[None, :] <= positions[:, None]) & (
        key_positions[None, :] >= starts[:, None]
    )
    scores = jnp.einsum("tgh,jh->tgj", query, keys, preferred_element_type=jnp.float32) * factor
    scores = jnp.where(visible[:, None, :], scores, -1e30)
    top = jnp.max(scores, axis=-1, keepdims=True)
    exps = jnp.where(visible[:, None, :], jnp.exp(scores - top), 0.0)
    probs = exps / jnp.sum(exps, axis=-1, keepdims=True)
    weights = probs.astype(jnp.bfloat16)
    grad_heads = attn_grad.reshape(count, GROUP, HEAD)
    prob_grad = jnp.einsum("tgh,jh->tgj", grad_heads, values, preferred_element_type=jnp.float32)
    inner = jnp.sum(probs * prob_grad, axis=-1, keepdims=True)
    score_grad = (probs * (prob_grad - inner) * factor).astype(jnp.bfloat16)
    query_grad = (
        jnp.einsum("tgj,jh->tgh", score_grad, keys, preferred_element_type=jnp.float32)
        .astype(jnp.bfloat16)
        .reshape(count, width)
    )
    key_part = jnp.einsum("tgj,tgh->jh", score_grad, query, preferred_element_type=jnp.float32)
    value_part = jnp.einsum("tgj,tgh->jh", weights, grad_heads, preferred_element_type=jnp.float32)
    kv_part = jnp.concatenate([key_part, value_part], axis=1).reshape(outer, INNER, count, 2 * HEAD)
    pieces = hidden.shape[1] // size
    query_all, hidden_cols = gather_and_scatter(
        query_grad.reshape(count, width // pieces, pieces).transpose(1, 0, 2), hidden, o, i
    )
    query_all = query_all.transpose(0, 2, 3, 1, 4).reshape(outer, INNER, count, width)
    hidden_cols = hidden_cols.reshape(size * count, -1)
    kv_grad = reduce_blocks(kv_part).astype(jnp.bfloat16)
    grad_all = jnp.concatenate([query_all, gather_blocks(kv_grad)], axis=-1).reshape(size * count, -1)
    input_term = contract_first(hidden_cols, grad_all).astype(jnp.bfloat16)
    block = contract_last(grad_all, up_input_weight[0])
    hidden_grad = gather_columns(block.astype(jnp.bfloat16).reshape(outer, INNER, count, -1), o, i)
    hidden_grad = hidden_grad.astype(jnp.float32)
    scaled = hidden_grad * upward_gain[0]
    input_grad = cotangent.astype(jnp.float32) + inverse_up * (
        scaled - unit_up * jnp.mean(scaled * unit_up, axis=-1, keepdims=True)
    )
    moved_grad = shifted(input_grad.astype(jnp.bfloat16), "section", 1)
    mirror_input = mirrored(input_term, "section")
    project_grads = (accum_input[0].astype(jnp.float32) + mirror_input.astype(jnp.float32)).astype(
        jnp.bfloat16
    )
    return (moved_grad[None], project_grads[None])


def solution(mesh):
    return jax.shard_map(
        per_device,
        mesh=mesh,
        in_specs=(
            P("section", "seq", None),
            P("section", "seq", None),
            P("section", "seq", None),
            P("section", "seq", None),
            P("section", None, "seq"),
            P("section", None),
            P("section", "seq", None),
            P("section", "seq"),
        ),
        out_specs=(P("section", "seq", None), P("section", "seq", None)),
        check_vma=False,
    )
```

```python
import jax
import jax.numpy as jnp
from jax import lax
from jax.sharding import PartitionSpec as P

HEAD = 128
GROUP = 4
INNER = 4


def shifted(value, axis, steps):
    count = lax.axis_size(axis)
    initial, last = (max(0, -steps), min(count, count - steps))
    return lax.ppermute(value, axis, [(source, source + steps) for source in range(initial, last)])


def mirrored(value, axis):
    count = lax.axis_size(axis)
    return lax.ppermute(value, axis, [(source, count - 1 - source) for source in range(count)])


def seq_pairs(shift, level):
    size = lax.axis_size("seq")
    outer = size // INNER
    if level == 0:
        return [(o * INNER + i, o * INNER + (i + shift) % INNER) for o in range(outer) for i in range(INNER)]
    return [(o * INNER + i, ((o + shift) % outer) * INNER + i) for o in range(outer) for i in range(INNER)]


def gather_blocks(x):
    outer = lax.axis_size("seq") // INNER
    first = jnp.stack([x] + [lax.ppermute(x, "seq", seq_pairs(k, 0)) for k in range(1, INNER)])
    return jnp.stack([first] + [lax.ppermute(first, "seq", seq_pairs(k, 1)) for k in range(1, outer)])


def reduce_blocks(y):
    outer = lax.axis_size("seq") // INNER
    acc = y[0]
    for k in range(1, outer):
        acc = acc + lax.ppermute(y[k], "seq", seq_pairs(outer - k, 1))
    total = acc[0]
    for k in range(1, INNER):
        total = total + lax.ppermute(acc[k], "seq", seq_pairs(INNER - k, 0))
    return total


def gather_and_scatter(x, cols, o, i):
    outer = lax.axis_size("seq") // INNER
    n = x.shape[0]
    parts = cols.reshape(n, outer, INNER, -1).transpose(2, 1, 0, 3)
    first = [jnp.concatenate([x[None], parts[i]])]
    for k in range(1, INNER):
        piece = lax.dynamic_index_in_dim(parts, (i + k) % INNER, 0, keepdims=False)
        first.append(lax.ppermute(jnp.concatenate([x[None], piece]), "seq", seq_pairs(k, 0)))
    first = jnp.stack(first, axis=1)
    second = [first]
    for k in range(1, outer):
        piece = lax.dynamic_index_in_dim(first[1:], (o + k) % outer, 0, keepdims=False)
        second.append(lax.ppermute(jnp.concatenate([first[0], piece]), "seq", seq_pairs(k, 1)))
    gathered = jnp.stack([second[0][0]] + [s[:INNER] for s in second[1:]])
    scattered = jnp.stack([second[0][1 + o]] + [s[INNER:] for s in second[1:]])
    return gathered, scattered


def reduce_and_gather(partial, own):
    outer = lax.axis_size("seq") // INNER
    n, w = partial.shape[2], partial.shape[3]
    wire = own.dtype
    pieces = own.reshape(n, -1, w).transpose(1, 0, 2)
    acc = partial[0]
    for k in range(1, outer):
        acc = acc + lax.ppermute(partial[k].astype(wire), "seq", seq_pairs(outer - k, 1)).astype(acc.dtype)
    total = acc[0]
    rows = [pieces]
    for k in range(1, INNER):
        payload = jnp.concatenate([acc[INNER - k].astype(wire)[None], pieces])
        got = lax.ppermute(payload, "seq", seq_pairs(k, 0))
        total = total + got[0].astype(acc.dtype)
        rows.append(got[1:])
    reduced = total.astype(wire)
    sums = jnp.stack([reduced] + [lax.ppermute(reduced, "seq", seq_pairs(k, 0)) for k in range(1, INNER)])
    group = jnp.concatenate([jnp.stack(rows).reshape(-1, n, w), sums])
    full = jnp.stack([group] + [lax.ppermute(group, "seq", seq_pairs(k, 1)) for k in range(1, outer)])
    m = pieces.shape[0]
    rows_all = full[:, : INNER * m].reshape(outer, INNER, m, n, w).transpose(0, 1, 3, 2, 4).reshape(outer, INNER, n, m * w)
    return jnp.concatenate([rows_all, full[:, INNER * m :]], axis=-1)


def gather_columns(y, o, i):
    outer = lax.axis_size("seq") // INNER
    n, w = y.shape[2], y.shape[3]
    first = [y[0]]
    for k in range(1, outer):
        first.append(lax.ppermute(y[k], "seq", seq_pairs(outer - k, 1)))
    first = jnp.stack(first, axis=1)
    second = [first[0]]
    for k in range(1, INNER):
        second.append(lax.ppermute(first[k], "seq", seq_pairs(INNER - k, 0)))
    second = jnp.stack(second, axis=1)
    second = jnp.roll(jnp.roll(second, o, axis=0), i, axis=1)
    return second.transpose(2, 0, 1, 3).reshape(n, outer * INNER * w)


def contract_last(left, right):
    return lax.dot_general(
        left, right, (((1,), (1,)), ((), ())), preferred_element_type=jnp.float32
    )


def contract_first(left, right):
    return lax.dot_general(
        left, right, (((0,), (0,)), ((), ())), preferred_element_type=jnp.float32
    )


def normalize(values, gain):
    floats = values.astype(jnp.float32)
    inverse = lax.rsqrt(jnp.mean(floats * floats, axis=-1, keepdims=True) + 1e-05)
    unit = floats * inverse
    return (unit, inverse, unit * gain)


def per_device(
    up_activation,
    saved_projections,
    up_cotangent,
    up_input_weight,
    up_output_weight,
    upward_gain,
    accum_input,
    doc_starts,
):
    factor = HEAD ** (-0.5)
    width = GROUP * HEAD
    count = up_activation.shape[1]
    size = lax.axis_size("seq")
    outer = size // INNER
    me = lax.axis_index("seq")
    o, i = me // INNER, me % INNER
    first = me * count
    saved = saved_projections[0]
    cotangent = up_cotangent[0]
    unit_up, inverse_up, normed_up = normalize(up_activation[0], upward_gain[0])
    hidden = normed_up.astype(jnp.bfloat16)
    output_weight = lax.all_gather(up_output_weight[0], "seq", axis=1, tiled=True)
    key_value, hidden_cols = gather_and_scatter(saved[:, width:], hidden, o, i)
    key_value = key_value.reshape(size * count, 2 * HEAD)
    hidden_cols = hidden_cols.reshape(size * count, -1)
    keys = key_value[:, :HEAD]
    values = key_value[:, HEAD:]
    sources = (
        ((o - jnp.arange(outer, dtype=jnp.int32)) % outer)[:, None] * INNER
        + ((i - jnp.arange(INNER, dtype=jnp.int32)) % INNER)[None, :]
    ).reshape(size)
    key_positions = (sources[:, None] * count + jnp.arange(count, dtype=jnp.int32)[None, :]).reshape(-1)
    query = saved[:, :width].reshape(count, GROUP, HEAD)
    attn_grad = contract_last(cotangent, output_weight).astype(jnp.bfloat16)
    positions = first + jnp.arange(count, dtype=jnp.int32)
    starts = doc_starts[0]
    visible = (key_positions[None, :] <= positions[:, None]) & (
        key_positions[None, :] >= starts[:, None]
    )
    scores = jnp.einsum("tgh,jh->tgj", query, keys, preferred_element_type=jnp.float32) * factor
    scores = jnp.where(visible[:, None, :], scores, -1e30)
    top = jnp.max(scores, axis=-1, keepdims=True)
    exps = jnp.where(visible[:, None, :], jnp.exp(scores - top), 0.0)
    probs = exps / jnp.sum(exps, axis=-1, keepdims=True)
    weights = probs.astype(jnp.bfloat16)
    grad_heads = attn_grad.reshape(count, GROUP, HEAD)
    prob_grad = jnp.einsum("tgh,jh->tgj", grad_heads, values, preferred_element_type=jnp.float32)
    inner = jnp.sum(probs * prob_grad, axis=-1, keepdims=True)
    score_grad = (probs * (prob_grad - inner) * factor).astype(jnp.bfloat16)
    query_grad = (
        jnp.einsum("tgj,jh->tgh", score_grad, keys, preferred_element_type=jnp.float32)
        .astype(jnp.bfloat16)
        .reshape(count, width)
    )
    key_part = jnp.einsum("tgj,tgh->jh", score_grad, query, preferred_element_type=jnp.float32)
    value_part = jnp.einsum("tgj,tgh->jh", weights, grad_heads, preferred_element_type=jnp.float32)
    kv_part = jnp.concatenate([key_part, value_part], axis=1).reshape(outer, INNER, count, 2 * HEAD)
    grad_all = reduce_and_gather(kv_part, query_grad).reshape(size * count, -1)
    input_term = contract_first(hidden_cols, grad_all).astype(jnp.bfloat16)
    block = contract_last(grad_all, up_input_weight[0])
    hidden_grad = gather_columns(block.astype(jnp.bfloat16).reshape(outer, INNER, count, -1), o, i)
    hidden_grad = hidden_grad.astype(jnp.float32)
    scaled = hidden_grad * upward_gain[0]
    input_grad = cotangent.astype(jnp.float32) + inverse_up * (
        scaled - unit_up * jnp.mean(scaled * unit_up, axis=-1, keepdims=True)
    )
    moved_grad = shifted(input_grad.astype(jnp.bfloat16), "section", 1)
    mirror_input = mirrored(input_term, "section")
    project_grads = (accum_input[0].astype(jnp.float32) + mirror_input.astype(jnp.float32)).astype(
        jnp.bfloat16
    )
    return (moved_grad[None], project_grads[None])


def solution(mesh):
    return jax.shard_map(
        per_device,
        mesh=mesh,
        in_specs=(
            P("section", "seq", None),
            P("section", "seq", None),
            P("section", "seq", None),
            P("section", "seq", None),
            P("section", None, "seq"),
            P("section", None),
            P("section", "seq", None),
            P("section", "seq"),
        ),
        out_specs=(P("section", "seq", None), P("section", "seq", None)),
        check_vma=False,
    )
```

```python
import jax
import jax.numpy as jnp
from jax import lax
from jax.sharding import PartitionSpec as P

HEAD = 128
GROUP = 4
INNER = 4


def shifted(value, axis, steps):
    count = lax.axis_size(axis)
    initial, last = (max(0, -steps), min(count, count - steps))
    return lax.ppermute(value, axis, [(source, source + steps) for source in range(initial, last)])


def mirrored(value, axis):
    count = lax.axis_size(axis)
    return lax.ppermute(value, axis, [(source, count - 1 - source) for source in range(count)])


def seq_pairs(shift, level):
    size = lax.axis_size("seq")
    outer = size // INNER
    if level == 0:
        return [(o * INNER + i, o * INNER + (i + shift) % INNER) for o in range(outer) for i in range(INNER)]
    return [(o * INNER + i, ((o + shift) % outer) * INNER + i) for o in range(outer) for i in range(INNER)]


def gather_blocks(x):
    outer = lax.axis_size("seq") // INNER
    first = jnp.stack([x] + [lax.ppermute(x, "seq", seq_pairs(k, 0)) for k in range(1, INNER)])
    return jnp.stack([first] + [lax.ppermute(first, "seq", seq_pairs(k, 1)) for k in range(1, outer)])


def reduce_blocks(y, wire):
    outer = lax.axis_size("seq") // INNER
    acc = y[0]
    for k in range(1, outer):
        acc = acc + lax.ppermute(y[k].astype(wire), "seq", seq_pairs(outer - k, 1)).astype(y.dtype)
    total = acc[0]
    for k in range(1, INNER):
        total = total + lax.ppermute(acc[k].astype(wire), "seq", seq_pairs(INNER - k, 0)).astype(y.dtype)
    return total


def gather_and_scatter(x, cols, o, i):
    outer = lax.axis_size("seq") // INNER
    m, n, w = x.shape
    parts = cols.reshape(n, outer, INNER, w).transpose(2, 1, 0, 3)
    first = [jnp.concatenate([x, parts[i]])]
    for k in range(1, INNER):
        piece = lax.dynamic_index_in_dim(parts, (i + k) % INNER, 0, keepdims=False)
        first.append(lax.ppermute(jnp.concatenate([x, piece]), "seq", seq_pairs(k, 0)))
    first = jnp.stack(first, axis=1)
    own, rest = first[:m], first[m:]
    second = []
    for k in range(1, outer):
        piece = lax.dynamic_index_in_dim(rest, (o + k) % outer, 0, keepdims=False)
        payload = jnp.concatenate([own.reshape(m * INNER, n, w), piece])
        second.append(lax.ppermute(payload, "seq", seq_pairs(k, 1)))
    gathered = jnp.stack([own] + [s[: m * INNER].reshape(m, INNER, n, w) for s in second])
    scattered = jnp.stack([lax.dynamic_index_in_dim(rest, o, 0, keepdims=False)] + [s[m * INNER :] for s in second])
    return gathered, scattered


def gather_columns(y, o, i):
    outer = lax.axis_size("seq") // INNER
    n, w = y.shape[2], y.shape[3]
    first = [y[0]]
    for k in range(1, outer):
        first.append(lax.ppermute(y[k], "seq", seq_pairs(outer - k, 1)))
    first = jnp.stack(first, axis=1)
    second = [first[0]]
    for k in range(1, INNER):
        second.append(lax.ppermute(first[k], "seq", seq_pairs(INNER - k, 0)))
    second = jnp.stack(second, axis=1)
    second = jnp.roll(jnp.roll(second, o, axis=0), i, axis=1)
    return second.transpose(2, 0, 1, 3).reshape(n, outer * INNER * w)


def contract_last(left, right):
    return lax.dot_general(
        left, right, (((1,), (1,)), ((), ())), preferred_element_type=jnp.float32
    )


def contract_first(left, right):
    return lax.dot_general(
        left, right, (((0,), (0,)), ((), ())), preferred_element_type=jnp.float32
    )


def normalize(values, gain):
    floats = values.astype(jnp.float32)
    inverse = lax.rsqrt(jnp.mean(floats * floats, axis=-1, keepdims=True) + 1e-05)
    unit = floats * inverse
    return (unit, inverse, unit * gain)


def per_device(
    up_activation,
    saved_projections,
    up_cotangent,
    up_input_weight,
    up_output_weight,
    upward_gain,
    accum_input,
    doc_starts,
):
    factor = HEAD ** (-0.5)
    width = GROUP * HEAD
    count = up_activation.shape[1]
    size = lax.axis_size("seq")
    outer = size // INNER
    me = lax.axis_index("seq")
    o, i = me // INNER, me % INNER
    first = me * count
    saved = saved_projections[0]
    cotangent = up_cotangent[0]
    unit_up, inverse_up, normed_up = normalize(up_activation[0], upward_gain[0])
    hidden = normed_up.astype(jnp.bfloat16)
    output_weight = lax.all_gather(up_output_weight[0], "seq", axis=1, tiled=True)
    pieces = hidden.shape[1] // size
    kv_weight = up_input_weight[0][:, width:]
    riders = jnp.concatenate(
        [saved[None, :, width:], kv_weight.reshape(-1, count, pieces)]
    )
    gathered, hidden_cols = gather_and_scatter(riders, hidden, o, i)
    key_value = gathered[:, 0].reshape(size * count, 2 * HEAD)
    hidden_cols = hidden_cols.reshape(size * count, -1)
    kv_weight_all = gathered[:, 1:].transpose(0, 2, 1, 3, 4)
    kv_weight_all = jnp.take(kv_weight_all, (o - jnp.arange(outer)) % outer, axis=0)
    kv_weight_all = jnp.take(kv_weight_all, (i - jnp.arange(INNER)) % INNER, axis=1)
    kv_weight_all = kv_weight_all.reshape(-1, 2 * HEAD)
    keys = key_value[:, :HEAD]
    values = key_value[:, HEAD:]
    sources = (
        ((o - jnp.arange(outer, dtype=jnp.int32)) % outer)[:, None] * INNER
        + ((i - jnp.arange(INNER, dtype=jnp.int32)) % INNER)[None, :]
    ).reshape(size)
    key_positions = (sources[:, None] * count + jnp.arange(count, dtype=jnp.int32)[None, :]).reshape(-1)
    query = saved[:, :width].reshape(count, GROUP, HEAD)
    attn_grad = contract_last(cotangent, output_weight).astype(jnp.bfloat16)
    positions = first + jnp.arange(count, dtype=jnp.int32)
    starts = doc_starts[0]
    visible = (key_positions[None, :] <= positions[:, None]) & (
        key_positions[None, :] >= starts[:, None]
    )
    scores = jnp.einsum("tgh,jh->tgj", query, keys, preferred_element_type=jnp.float32) * factor
    scores = jnp.where(visible[:, None, :], scores, -1e30)
    top = jnp.max(scores, axis=-1, keepdims=True)
    exps = jnp.where(visible[:, None, :], jnp.exp(scores - top), 0.0)
    probs = exps / jnp.sum(exps, axis=-1, keepdims=True)
    weights = probs.astype(jnp.bfloat16)
    grad_heads = attn_grad.reshape(count, GROUP, HEAD)
    prob_grad = jnp.einsum("tgh,jh->tgj", grad_heads, values, preferred_element_type=jnp.float32)
    inner = jnp.sum(probs * prob_grad, axis=-1, keepdims=True)
    score_grad = (probs * (prob_grad - inner) * factor).astype(jnp.bfloat16)
    query_grad = (
        jnp.einsum("tgj,jh->tgh", score_grad, keys, preferred_element_type=jnp.float32)
        .astype(jnp.bfloat16)
        .reshape(count, width)
    )
    key_part = jnp.einsum("tgj,tgh->jh", score_grad, query, preferred_element_type=jnp.float32)
    value_part = jnp.einsum("tgj,tgh->jh", weights, grad_heads, preferred_element_type=jnp.float32)
    kv_part = jnp.concatenate([key_part, value_part], axis=1).reshape(outer, INNER, count, 2 * HEAD)
    query_all = gather_blocks(query_grad)
    kv_grad = reduce_blocks(kv_part, jnp.bfloat16).astype(jnp.bfloat16)
    grad_all = jnp.concatenate([query_all, gather_blocks(kv_grad)], axis=-1).reshape(size * count, -1)
    input_term = contract_first(hidden_cols, grad_all).astype(jnp.bfloat16)
    block = contract_last(query_all.reshape(size * count, -1), up_input_weight[0][:, :width])
    hidden_grad = gather_columns(block.astype(jnp.bfloat16).reshape(outer, INNER, count, -1), o, i)
    hidden_grad = hidden_grad.astype(jnp.float32) + contract_last(kv_grad, kv_weight_all)
    scaled = hidden_grad * upward_gain[0]
    input_grad = cotangent.astype(jnp.float32) + inverse_up * (
        scaled - unit_up * jnp.mean(scaled * unit_up, axis=-1, keepdims=True)
    )
    moved_grad = shifted(input_grad.astype(jnp.bfloat16), "section", 1)
    mirror_input = mirrored(input_term, "section")
    project_grads = (accum_input[0].astype(jnp.float32) + mirror_input.astype(jnp.float32)).astype(
        jnp.bfloat16
    )
    return (moved_grad[None], project_grads[None])


def solution(mesh):
    return jax.shard_map(
        per_device,
        mesh=mesh,
        in_specs=(
            P("section", "seq", None),
            P("section", "seq", None),
            P("section", "seq", None),
            P("section", "seq", None),
            P("section", None, "seq"),
            P("section", None),
            P("section", "seq", None),
            P("section", "seq"),
        ),
        out_specs=(P("section", "seq", None), P("section", "seq", None)),
        check_vma=False,
    )
```

```python
import jax
import jax.numpy as jnp
from jax import lax
from jax.sharding import PartitionSpec as P

HEAD = 128
GROUP = 4
INNER = 4


def shifted(value, axis, steps):
    count = lax.axis_size(axis)
    initial, last = (max(0, -steps), min(count, count - steps))
    return lax.ppermute(value, axis, [(source, source + steps) for source in range(initial, last)])


def mirrored(value, axis):
    count = lax.axis_size(axis)
    return lax.ppermute(value, axis, [(source, count - 1 - source) for source in range(count)])


def seq_pairs(shift, level):
    size = lax.axis_size("seq")
    outer = size // INNER
    if level == 0:
        return [(o * INNER + i, o * INNER + (i + shift) % INNER) for o in range(outer) for i in range(INNER)]
    return [(o * INNER + i, ((o + shift) % outer) * INNER + i) for o in range(outer) for i in range(INNER)]


def gather_blocks(x):
    outer = lax.axis_size("seq") // INNER
    first = jnp.stack([x] + [lax.ppermute(x, "seq", seq_pairs(k, 0)) for k in range(1, INNER)])
    return jnp.stack([first] + [lax.ppermute(first, "seq", seq_pairs(k, 1)) for k in range(1, outer)])


def reduce_blocks(y, wire):
    outer = lax.axis_size("seq") // INNER
    acc = y[0]
    for k in range(1, outer):
        acc = acc + lax.ppermute(y[k].astype(wire), "seq", seq_pairs(outer - k, 1)).astype(y.dtype)
    total = acc[0]
    for k in range(1, INNER):
        total = total + lax.ppermute(acc[k].astype(wire), "seq", seq_pairs(INNER - k, 0)).astype(y.dtype)
    return total


def gather_and_scatter(x, cols, o, i):
    outer = lax.axis_size("seq") // INNER
    m, n, w = x.shape
    parts = cols.reshape(n, outer, INNER, w).transpose(2, 1, 0, 3)
    first = [jnp.concatenate([x, parts[i]])]
    for k in range(1, INNER):
        piece = lax.dynamic_index_in_dim(parts, (i + k) % INNER, 0, keepdims=False)
        first.append(lax.ppermute(jnp.concatenate([x, piece]), "seq", seq_pairs(k, 0)))
    first = jnp.stack(first, axis=1)
    own, rest = first[:m], first[m:]
    second = []
    for k in range(1, outer):
        piece = lax.dynamic_index_in_dim(rest, (o + k) % outer, 0, keepdims=False)
        payload = jnp.concatenate([own.reshape(m * INNER, n, w), piece])
        second.append(lax.ppermute(payload, "seq", seq_pairs(k, 1)))
    gathered = jnp.stack([own] + [s[: m * INNER].reshape(m, INNER, n, w) for s in second])
    scattered = jnp.stack([lax.dynamic_index_in_dim(rest, o, 0, keepdims=False)] + [s[m * INNER :] for s in second])
    return gathered, scattered


def gather_columns(y, o, i):
    outer = lax.axis_size("seq") // INNER
    n, w = y.shape[2], y.shape[3]
    first = [y[0]]
    for k in range(1, outer):
        first.append(lax.ppermute(y[k], "seq", seq_pairs(outer - k, 1)))
    first = jnp.stack(first, axis=1)
    second = [first[0]]
    for k in range(1, INNER):
        second.append(lax.ppermute(first[k], "seq", seq_pairs(INNER - k, 0)))
    second = jnp.stack(second, axis=1)
    second = jnp.roll(jnp.roll(second, o, axis=0), i, axis=1)
    return second.transpose(2, 0, 1, 3).reshape(n, outer * INNER * w)


def contract_last(left, right):
    return lax.dot_general(
        left, right, (((1,), (1,)), ((), ())), preferred_element_type=jnp.float32
    )


def contract_first(left, right):
    return lax.dot_general(
        left, right, (((0,), (0,)), ((), ())), preferred_element_type=jnp.float32
    )


def normalize(values, gain):
    floats = values.astype(jnp.float32)
    inverse = lax.rsqrt(jnp.mean(floats * floats, axis=-1, keepdims=True) + 1e-05)
    unit = floats * inverse
    return (unit, inverse, unit * gain)


def per_device(
    up_activation,
    saved_projections,
    up_cotangent,
    up_input_weight,
    up_output_weight,
    upward_gain,
    accum_input,
    doc_starts,
):
    factor = HEAD ** (-0.5)
    width = GROUP * HEAD
    count = up_activation.shape[1]
    size = lax.axis_size("seq")
    outer = size // INNER
    me = lax.axis_index("seq")
    o, i = me // INNER, me % INNER
    first = me * count
    saved = saved_projections[0]
    cotangent = up_cotangent[0]
    unit_up, inverse_up, normed_up = normalize(up_activation[0], upward_gain[0])
    hidden = normed_up.astype(jnp.bfloat16)
    output_weight = lax.all_gather(up_output_weight[0], "seq", axis=1, tiled=True)
    pieces = hidden.shape[1] // size
    kv_weight = up_input_weight[0][:, width:]
    riders = jnp.concatenate(
        [saved[None, :, width:], kv_weight.reshape(-1, count, pieces)]
    )
    gathered = gather_blocks(riders)
    key_value = gathered[:, :, 0].reshape(size * count, 2 * HEAD)
    kv_weight_all = gathered[:, :, 1:]
    kv_weight_all = jnp.take(kv_weight_all, (o - jnp.arange(outer)) % outer, axis=0)
    kv_weight_all = jnp.take(kv_weight_all, (i - jnp.arange(INNER)) % INNER, axis=1)
    kv_weight_all = kv_weight_all.reshape(-1, 2 * HEAD)
    keys = key_value[:, :HEAD]
    values = key_value[:, HEAD:]
    sources = (
        ((o - jnp.arange(outer, dtype=jnp.int32)) % outer)[:, None] * INNER
        + ((i - jnp.arange(INNER, dtype=jnp.int32)) % INNER)[None, :]
    ).reshape(size)
    key_positions = (sources[:, None] * count + jnp.arange(count, dtype=jnp.int32)[None, :]).reshape(-1)
    query = saved[:, :width].reshape(count, GROUP, HEAD)
    attn_grad = contract_last(cotangent, output_weight).astype(jnp.bfloat16)
    positions = first + jnp.arange(count, dtype=jnp.int32)
    starts = doc_starts[0]
    visible = (key_positions[None, :] <= positions[:, None]) & (
        key_positions[None, :] >= starts[:, None]
    )
    scores = jnp.einsum("tgh,jh->tgj", query, keys, preferred_element_type=jnp.float32) * factor
    scores = jnp.where(visible[:, None, :], scores, -1e30)
    top = jnp.max(scores, axis=-1, keepdims=True)
    exps = jnp.where(visible[:, None, :], jnp.exp(scores - top), 0.0)
    probs = exps / jnp.sum(exps, axis=-1, keepdims=True)
    weights = probs.astype(jnp.bfloat16)
    grad_heads = attn_grad.reshape(count, GROUP, HEAD)
    prob_grad = jnp.einsum("tgh,jh->tgj", grad_heads, values, preferred_element_type=jnp.float32)
    inner = jnp.sum(probs * prob_grad, axis=-1, keepdims=True)
    score_grad = (probs * (prob_grad - inner) * factor).astype(jnp.bfloat16)
    query_grad = (
        jnp.einsum("tgj,jh->tgh", score_grad, keys, preferred_element_type=jnp.float32)
        .astype(jnp.bfloat16)
        .reshape(count, width)
    )
    key_part = jnp.einsum("tgj,tgh->jh", score_grad, query, preferred_element_type=jnp.float32)
    value_part = jnp.einsum("tgj,tgh->jh", weights, grad_heads, preferred_element_type=jnp.float32)
    kv_part = jnp.concatenate([key_part, value_part], axis=1).reshape(outer, INNER, count, 2 * HEAD)
    query_all = gather_blocks(query_grad)
    kv_grad = reduce_blocks(kv_part, jnp.bfloat16).astype(jnp.bfloat16)
    kv_all, hidden_cols = gather_and_scatter(kv_grad[None], hidden, o, i)
    hidden_cols = hidden_cols.reshape(size * count, -1)
    grad_all = jnp.concatenate([query_all, kv_all[:, 0]], axis=-1).reshape(size * count, -1)
    input_term = contract_first(hidden_cols, grad_all).astype(jnp.bfloat16)
    block = contract_last(query_all.reshape(size * count, -1), up_input_weight[0][:, :width])
    hidden_grad = gather_columns(block.astype(jnp.bfloat16).reshape(outer, INNER, count, -1), o, i)
    hidden_grad = hidden_grad.astype(jnp.float32) + contract_last(kv_grad, kv_weight_all)
    scaled = hidden_grad * upward_gain[0]
    input_grad = cotangent.astype(jnp.float32) + inverse_up * (
        scaled - unit_up * jnp.mean(scaled * unit_up, axis=-1, keepdims=True)
    )
    moved_grad = shifted(input_grad.astype(jnp.bfloat16), "section", 1)
    mirror_input = mirrored(input_term, "section")
    project_grads = (accum_input[0].astype(jnp.float32) + mirror_input.astype(jnp.float32)).astype(
        jnp.bfloat16
    )
    return (moved_grad[None], project_grads[None])


def solution(mesh):
    return jax.shard_map(
        per_device,
        mesh=mesh,
        in_specs=(
            P("section", "seq", None),
            P("section", "seq", None),
            P("section", "seq", None),
            P("section", "seq", None),
            P("section", None, "seq"),
            P("section", None),
            P("section", "seq", None),
            P("section", "seq"),
        ),
        out_specs=(P("section", "seq", None), P("section", "seq", None)),
        check_vma=False,
    )
```

```python
import jax
import jax.numpy as jnp
from jax import lax
from jax.sharding import PartitionSpec as P

HEAD = 128
GROUP = 4
INNER = 4


def shifted(value, axis, steps):
    count = lax.axis_size(axis)
    initial, last = (max(0, -steps), min(count, count - steps))
    return lax.ppermute(value, axis, [(source, source + steps) for source in range(initial, last)])


def mirrored(value, axis):
    count = lax.axis_size(axis)
    return lax.ppermute(value, axis, [(source, count - 1 - source) for source in range(count)])


def seq_pairs(shift, level):
    size = lax.axis_size("seq")
    outer = size // INNER
    if level == 0:
        return [(o * INNER + i, o * INNER + (i + shift) % INNER) for o in range(outer) for i in range(INNER)]
    return [(o * INNER + i, ((o + shift) % outer) * INNER + i) for o in range(outer) for i in range(INNER)]


def gather_blocks(x):
    outer = lax.axis_size("seq") // INNER
    first = jnp.stack([x] + [lax.ppermute(x, "seq", seq_pairs(k, 0)) for k in range(1, INNER)])
    return jnp.stack([first] + [lax.ppermute(first, "seq", seq_pairs(k, 1)) for k in range(1, outer)])


def reduce_blocks(y, wire):
    outer = lax.axis_size("seq") // INNER
    acc = y[0]
    for k in range(1, outer):
        acc = acc + lax.ppermute(y[k].astype(wire), "seq", seq_pairs(outer - k, 1)).astype(y.dtype)
    total = acc[0]
    for k in range(1, INNER):
        total = total + lax.ppermute(acc[k].astype(wire), "seq", seq_pairs(INNER - k, 0)).astype(y.dtype)
    return total


def gather_and_scatter(x, cols, o, i):
    outer = lax.axis_size("seq") // INNER
    m, n, w = x.shape
    parts = cols.reshape(n, outer, INNER, w).transpose(2, 1, 0, 3)
    first = [jnp.concatenate([x, parts[i]])]
    for k in range(1, INNER):
        piece = lax.dynamic_index_in_dim(parts, (i + k) % INNER, 0, keepdims=False)
        first.append(lax.ppermute(jnp.concatenate([x, piece]), "seq", seq_pairs(k, 0)))
    first = jnp.stack(first, axis=1)
    own, rest = first[:m], first[m:]
    second = []
    for k in range(1, outer):
        piece = lax.dynamic_index_in_dim(rest, (o + k) % outer, 0, keepdims=False)
        payload = jnp.concatenate([own.reshape(m * INNER, n, w), piece])
        second.append(lax.ppermute(payload, "seq", seq_pairs(k, 1)))
    gathered = jnp.stack([own] + [s[: m * INNER].reshape(m, INNER, n, w) for s in second])
    scattered = jnp.stack([lax.dynamic_index_in_dim(rest, o, 0, keepdims=False)] + [s[m * INNER :] for s in second])
    return gathered, scattered


def gather_columns(y, o, i):
    outer = lax.axis_size("seq") // INNER
    n, w = y.shape[2], y.shape[3]
    first = [y[0]]
    for k in range(1, outer):
        first.append(lax.ppermute(y[k], "seq", seq_pairs(outer - k, 1)))
    first = jnp.stack(first, axis=1)
    second = [first[0]]
    for k in range(1, INNER):
        second.append(lax.ppermute(first[k], "seq", seq_pairs(INNER - k, 0)))
    second = jnp.stack(second, axis=1)
    second = jnp.roll(jnp.roll(second, o, axis=0), i, axis=1)
    return second.transpose(2, 0, 1, 3).reshape(n, outer * INNER * w)


def contract_last(left, right):
    return lax.dot_general(
        left, right, (((1,), (1,)), ((), ())), preferred_element_type=jnp.float32
    )


def contract_first(left, right):
    return lax.dot_general(
        left, right, (((0,), (0,)), ((), ())), preferred_element_type=jnp.float32
    )


def normalize(values, gain):
    floats = values.astype(jnp.float32)
    inverse = lax.rsqrt(jnp.mean(floats * floats, axis=-1, keepdims=True) + 1e-05)
    unit = floats * inverse
    return (unit, inverse, unit * gain)


def per_device(
    up_activation,
    saved_projections,
    up_cotangent,
    up_input_weight,
    up_output_weight,
    upward_gain,
    accum_input,
    doc_starts,
):
    factor = HEAD ** (-0.5)
    width = GROUP * HEAD
    count = up_activation.shape[1]
    size = lax.axis_size("seq")
    outer = size // INNER
    me = lax.axis_index("seq")
    o, i = me // INNER, me % INNER
    first = me * count
    saved = saved_projections[0]
    cotangent = up_cotangent[0]
    unit_up, inverse_up, normed_up = normalize(up_activation[0], upward_gain[0])
    hidden = normed_up.astype(jnp.bfloat16)
    output_weight = lax.all_gather(up_output_weight[0], "seq", axis=1, tiled=True)
    key_value = gather_blocks(saved[:, width:]).reshape(size * count, 2 * HEAD)
    kv_weight_all = lax.all_gather(up_input_weight[0][:, width:], "seq", axis=0, tiled=True)
    keys = key_value[:, :HEAD]
    values = key_value[:, HEAD:]
    sources = (
        ((o - jnp.arange(outer, dtype=jnp.int32)) % outer)[:, None] * INNER
        + ((i - jnp.arange(INNER, dtype=jnp.int32)) % INNER)[None, :]
    ).reshape(size)
    key_positions = (sources[:, None] * count + jnp.arange(count, dtype=jnp.int32)[None, :]).reshape(-1)
    query = saved[:, :width].reshape(count, GROUP, HEAD)
    attn_grad = contract_last(cotangent, output_weight).astype(jnp.bfloat16)
    positions = first + jnp.arange(count, dtype=jnp.int32)
    starts = doc_starts[0]
    visible = (key_positions[None, :] <= positions[:, None]) & (
        key_positions[None, :] >= starts[:, None]
    )
    scores = jnp.einsum("tgh,jh->tgj", query, keys, preferred_element_type=jnp.float32) * factor
    scores = jnp.where(visible[:, None, :], scores, -1e30)
    top = jnp.max(scores, axis=-1, keepdims=True)
    exps = jnp.where(visible[:, None, :], jnp.exp(scores - top), 0.0)
    probs = exps / jnp.sum(exps, axis=-1, keepdims=True)
    weights = probs.astype(jnp.bfloat16)
    grad_heads = attn_grad.reshape(count, GROUP, HEAD)
    prob_grad = jnp.einsum("tgh,jh->tgj", grad_heads, values, preferred_element_type=jnp.float32)
    inner = jnp.sum(probs * prob_grad, axis=-1, keepdims=True)
    score_grad = (probs * (prob_grad - inner) * factor).astype(jnp.bfloat16)
    query_grad = (
        jnp.einsum("tgj,jh->tgh", score_grad, keys, preferred_element_type=jnp.float32)
        .astype(jnp.bfloat16)
        .reshape(count, width)
    )
    key_part = jnp.einsum("tgj,tgh->jh", score_grad, query, preferred_element_type=jnp.float32)
    value_part = jnp.einsum("tgj,tgh->jh", weights, grad_heads, preferred_element_type=jnp.float32)
    kv_part = jnp.concatenate([key_part, value_part], axis=1).reshape(outer, INNER, count, 2 * HEAD)
    query_all = gather_blocks(query_grad)
    kv_grad = reduce_blocks(kv_part, jnp.bfloat16).astype(jnp.bfloat16)
    kv_all, hidden_cols = gather_and_scatter(kv_grad[None], hidden, o, i)
    hidden_cols = hidden_cols.reshape(size * count, -1)
    grad_all = jnp.concatenate([query_all, kv_all[:, 0]], axis=-1).reshape(size * count, -1)
    input_term = contract_first(hidden_cols, grad_all).astype(jnp.bfloat16)
    block = contract_last(query_all.reshape(size * count, -1), up_input_weight[0][:, :width])
    hidden_grad = gather_columns(block.astype(jnp.bfloat16).reshape(outer, INNER, count, -1), o, i)
    hidden_grad = hidden_grad.astype(jnp.float32) + contract_last(kv_grad, kv_weight_all)
    scaled = hidden_grad * upward_gain[0]
    input_grad = cotangent.astype(jnp.float32) + inverse_up * (
        scaled - unit_up * jnp.mean(scaled * unit_up, axis=-1, keepdims=True)
    )
    moved_grad = shifted(input_grad.astype(jnp.bfloat16), "section", 1)
    mirror_input = mirrored(input_term, "section")
    project_grads = (accum_input[0].astype(jnp.float32) + mirror_input.astype(jnp.float32)).astype(
        jnp.bfloat16
    )
    return (moved_grad[None], project_grads[None])


def solution(mesh):
    return jax.shard_map(
        per_device,
        mesh=mesh,
        in_specs=(
            P("section", "seq", None),
            P("section", "seq", None),
            P("section", "seq", None),
            P("section", "seq", None),
            P("section", None, "seq"),
            P("section", None),
            P("section", "seq", None),
            P("section", "seq"),
        ),
        out_specs=(P("section", "seq", None), P("section", "seq", None)),
        check_vma=False,
    )
```

```python
import jax
import jax.numpy as jnp
from jax import lax
from jax.sharding import PartitionSpec as P

HEAD = 128
GROUP = 4
INNER = 4


def shifted(value, axis, steps):
    count = lax.axis_size(axis)
    initial, last = (max(0, -steps), min(count, count - steps))
    return lax.ppermute(value, axis, [(source, source + steps) for source in range(initial, last)])


def mirrored(value, axis):
    count = lax.axis_size(axis)
    return lax.ppermute(value, axis, [(source, count - 1 - source) for source in range(count)])


def seq_pairs(shift, level):
    size = lax.axis_size("seq")
    outer = size // INNER
    if level == 0:
        return [(o * INNER + i, o * INNER + (i + shift) % INNER) for o in range(outer) for i in range(INNER)]
    return [(o * INNER + i, ((o + shift) % outer) * INNER + i) for o in range(outer) for i in range(INNER)]


def gather_blocks(x):
    outer = lax.axis_size("seq") // INNER
    first = jnp.stack([x] + [lax.ppermute(x, "seq", seq_pairs(k, 0)) for k in range(1, INNER)])
    return jnp.stack([first] + [lax.ppermute(first, "seq", seq_pairs(k, 1)) for k in range(1, outer)])


def reduce_blocks(y, wire):
    outer = lax.axis_size("seq") // INNER
    acc = y[0]
    for k in range(1, outer):
        acc = acc + lax.ppermute(y[k].astype(wire), "seq", seq_pairs(outer - k, 1)).astype(y.dtype)
    total = acc[0]
    for k in range(1, INNER):
        total = total + lax.ppermute(acc[k].astype(wire), "seq", seq_pairs(INNER - k, 0)).astype(y.dtype)
    return total


def gather_and_scatter(x, cols, o, i):
    outer = lax.axis_size("seq") // INNER
    m, n, w = x.shape
    parts = cols.reshape(n, outer, INNER, w).transpose(2, 1, 0, 3)
    first = [jnp.concatenate([x, parts[i]])]
    for k in range(1, INNER):
        piece = lax.dynamic_index_in_dim(parts, (i + k) % INNER, 0, keepdims=False)
        first.append(lax.ppermute(jnp.concatenate([x, piece]), "seq", seq_pairs(k, 0)))
    first = jnp.stack(first, axis=1)
    own, rest = first[:m], first[m:]
    second = []
    for k in range(1, outer):
        piece = lax.dynamic_index_in_dim(rest, (o + k) % outer, 0, keepdims=False)
        payload = jnp.concatenate([own.reshape(m * INNER, n, w), piece])
        second.append(lax.ppermute(payload, "seq", seq_pairs(k, 1)))
    gathered = jnp.stack([own] + [s[: m * INNER].reshape(m, INNER, n, w) for s in second])
    scattered = jnp.stack([lax.dynamic_index_in_dim(rest, o, 0, keepdims=False)] + [s[m * INNER :] for s in second])
    return gathered, scattered


def gather_columns(y, o, i):
    outer = lax.axis_size("seq") // INNER
    n, w = y.shape[2], y.shape[3]
    first = [y[0]]
    for k in range(1, outer):
        first.append(lax.ppermute(y[k], "seq", seq_pairs(outer - k, 1)))
    first = jnp.stack(first, axis=1)
    second = [first[0]]
    for k in range(1, INNER):
        second.append(lax.ppermute(first[k], "seq", seq_pairs(INNER - k, 0)))
    second = jnp.stack(second, axis=1)
    second = jnp.roll(jnp.roll(second, o, axis=0), i, axis=1)
    return second.transpose(2, 0, 1, 3).reshape(n, outer * INNER * w)


def contract_last(left, right):
    return lax.dot_general(
        left, right, (((1,), (1,)), ((), ())), preferred_element_type=jnp.float32
    )


def contract_first(left, right):
    return lax.dot_general(
        left, right, (((0,), (0,)), ((), ())), preferred_element_type=jnp.float32
    )


def normalize(values, gain):
    floats = values.astype(jnp.float32)
    inverse = lax.rsqrt(jnp.mean(floats * floats, axis=-1, keepdims=True) + 1e-05)
    unit = floats * inverse
    return (unit, inverse, unit * gain)


def per_device(
    up_activation,
    saved_projections,
    up_cotangent,
    up_input_weight,
    up_output_weight,
    upward_gain,
    accum_input,
    doc_starts,
):
    factor = HEAD ** (-0.5)
    width = GROUP * HEAD
    count = up_activation.shape[1]
    size = lax.axis_size("seq")
    outer = size // INNER
    me = lax.axis_index("seq")
    o, i = me // INNER, me % INNER
    first = me * count
    saved = saved_projections[0]
    cotangent = up_cotangent[0]
    unit_up, inverse_up, normed_up = normalize(up_activation[0], upward_gain[0])
    hidden = normed_up.astype(jnp.bfloat16)
    split = width - HEAD
    output_main = lax.all_gather(up_output_weight[0][:split], "seq", axis=1, tiled=True)
    riders = gather_blocks(jnp.stack([saved[:, width:], up_output_weight[0][split:]]))
    key_value = riders[:, :, 0].reshape(size * count, 2 * HEAD)
    output_tail = jnp.take(riders[:, :, 1], (o - jnp.arange(outer)) % outer, axis=0)
    output_tail = jnp.take(output_tail, (i - jnp.arange(INNER)) % INNER, axis=1)
    output_tail = output_tail.transpose(2, 0, 1, 3).reshape(HEAD, -1)
    kv_weight_all = lax.all_gather(up_input_weight[0][:, width:], "seq", axis=0, tiled=True)
    keys = key_value[:, :HEAD]
    values = key_value[:, HEAD:]
    sources = (
        ((o - jnp.arange(outer, dtype=jnp.int32)) % outer)[:, None] * INNER
        + ((i - jnp.arange(INNER, dtype=jnp.int32)) % INNER)[None, :]
    ).reshape(size)
    key_positions = (sources[:, None] * count + jnp.arange(count, dtype=jnp.int32)[None, :]).reshape(-1)
    query = saved[:, :width].reshape(count, GROUP, HEAD)
    attn_grad = jnp.concatenate(
        [contract_last(cotangent, output_main), contract_last(cotangent, output_tail)], axis=1
    ).astype(jnp.bfloat16)
    positions = first + jnp.arange(count, dtype=jnp.int32)
    starts = doc_starts[0]
    visible = (key_positions[None, :] <= positions[:, None]) & (
        key_positions[None, :] >= starts[:, None]
    )
    scores = jnp.einsum("tgh,jh->tgj", query, keys, preferred_element_type=jnp.float32) * factor
    scores = jnp.where(visible[:, None, :], scores, -1e30)
    top = jnp.max(scores, axis=-1, keepdims=True)
    exps = jnp.where(visible[:, None, :], jnp.exp(scores - top), 0.0)
    probs = exps / jnp.sum(exps, axis=-1, keepdims=True)
    weights = probs.astype(jnp.bfloat16)
    grad_heads = attn_grad.reshape(count, GROUP, HEAD)
    prob_grad = jnp.einsum("tgh,jh->tgj", grad_heads, values, preferred_element_type=jnp.float32)
    inner = jnp.sum(probs * prob_grad, axis=-1, keepdims=True)
    score_grad = (probs * (prob_grad - inner) * factor).astype(jnp.bfloat16)
    query_grad = (
        jnp.einsum("tgj,jh->tgh", score_grad, keys, preferred_element_type=jnp.float32)
        .astype(jnp.bfloat16)
        .reshape(count, width)
    )
    key_part = jnp.einsum("tgj,tgh->jh", score_grad, query, preferred_element_type=jnp.float32)
    value_part = jnp.einsum("tgj,tgh->jh", weights, grad_heads, preferred_element_type=jnp.float32)
    kv_part = jnp.concatenate([key_part, value_part], axis=1).reshape(outer, INNER, count, 2 * HEAD)
    query_all = gather_blocks(query_grad)
    kv_grad = reduce_blocks(kv_part, jnp.bfloat16).astype(jnp.bfloat16)
    kv_all, hidden_cols = gather_and_scatter(kv_grad[None], hidden, o, i)
    hidden_cols = hidden_cols.reshape(size * count, -1)
    grad_all = jnp.concatenate([query_all, kv_all[:, 0]], axis=-1).reshape(size * count, -1)
    input_term = contract_first(hidden_cols, grad_all).astype(jnp.bfloat16)
    block = contract_last(query_all.reshape(size * count, -1), up_input_weight[0][:, :width])
    hidden_grad = gather_columns(block.astype(jnp.bfloat16).reshape(outer, INNER, count, -1), o, i)
    hidden_grad = hidden_grad.astype(jnp.float32) + contract_last(kv_grad, kv_weight_all)
    scaled = hidden_grad * upward_gain[0]
    input_grad = cotangent.astype(jnp.float32) + inverse_up * (
        scaled - unit_up * jnp.mean(scaled * unit_up, axis=-1, keepdims=True)
    )
    moved_grad = shifted(input_grad.astype(jnp.bfloat16), "section", 1)
    mirror_input = mirrored(input_term, "section")
    project_grads = (accum_input[0].astype(jnp.float32) + mirror_input.astype(jnp.float32)).astype(
        jnp.bfloat16
    )
    return (moved_grad[None], project_grads[None])


def solution(mesh):
    return jax.shard_map(
        per_device,
        mesh=mesh,
        in_specs=(
            P("section", "seq", None),
            P("section", "seq", None),
            P("section", "seq", None),
            P("section", "seq", None),
            P("section", None, "seq"),
            P("section", None),
            P("section", "seq", None),
            P("section", "seq"),
        ),
        out_specs=(P("section", "seq", None), P("section", "seq", None)),
        check_vma=False,
    )
```

```python
import jax
import jax.numpy as jnp
from jax import lax
from jax.sharding import PartitionSpec as P

HEAD = 128
GROUP = 4
INNER = 4


def shifted(value, axis, steps):
    count = lax.axis_size(axis)
    initial, last = (max(0, -steps), min(count, count - steps))
    return lax.ppermute(value, axis, [(source, source + steps) for source in range(initial, last)])


def mirrored(value, axis):
    count = lax.axis_size(axis)
    return lax.ppermute(value, axis, [(source, count - 1 - source) for source in range(count)])


def seq_pairs(shift, level):
    size = lax.axis_size("seq")
    outer = size // INNER
    if level == 0:
        return [(o * INNER + i, o * INNER + (i + shift) % INNER) for o in range(outer) for i in range(INNER)]
    return [(o * INNER + i, ((o + shift) % outer) * INNER + i) for o in range(outer) for i in range(INNER)]


def gather_blocks(x):
    outer = lax.axis_size("seq") // INNER
    first = jnp.stack([x] + [lax.ppermute(x, "seq", seq_pairs(k, 0)) for k in range(1, INNER)])
    return jnp.stack([first] + [lax.ppermute(first, "seq", seq_pairs(k, 1)) for k in range(1, outer)])


def reduce_blocks(y, wire):
    outer = lax.axis_size("seq") // INNER
    acc = y[0]
    for k in range(1, outer):
        acc = acc + lax.ppermute(y[k].astype(wire), "seq", seq_pairs(outer - k, 1)).astype(y.dtype)
    total = acc[0]
    for k in range(1, INNER):
        total = total + lax.ppermute(acc[k].astype(wire), "seq", seq_pairs(INNER - k, 0)).astype(y.dtype)
    return total


def gather_and_scatter(x, cols, o, i):
    outer = lax.axis_size("seq") // INNER
    m, n, w = x.shape
    parts = cols.reshape(n, outer, INNER, w).transpose(2, 1, 0, 3)
    first = [jnp.concatenate([x, parts[i]])]
    for k in range(1, INNER):
        piece = lax.dynamic_index_in_dim(parts, (i + k) % INNER, 0, keepdims=False)
        first.append(lax.ppermute(jnp.concatenate([x, piece]), "seq", seq_pairs(k, 0)))
    first = jnp.stack(first, axis=1)
    own, rest = first[:m], first[m:]
    second = []
    for k in range(1, outer):
        piece = lax.dynamic_index_in_dim(rest, (o + k) % outer, 0, keepdims=False)
        payload = jnp.concatenate([own.reshape(m * INNER, n, w), piece])
        second.append(lax.ppermute(payload, "seq", seq_pairs(k, 1)))
    gathered = jnp.stack([own] + [s[: m * INNER].reshape(m, INNER, n, w) for s in second])
    scattered = jnp.stack([lax.dynamic_index_in_dim(rest, o, 0, keepdims=False)] + [s[m * INNER :] for s in second])
    return gathered, scattered


def gather_columns(y, o, i):
    outer = lax.axis_size("seq") // INNER
    n, w = y.shape[2], y.shape[3]
    first = [y[0]]
    for k in range(1, outer):
        first.append(lax.ppermute(y[k], "seq", seq_pairs(outer - k, 1)))
    first = jnp.stack(first, axis=1)
    second = [first[0]]
    for k in range(1, INNER):
        second.append(lax.ppermute(first[k], "seq", seq_pairs(INNER - k, 0)))
    second = jnp.stack(second, axis=1)
    second = jnp.roll(jnp.roll(second, o, axis=0), i, axis=1)
    return second.transpose(2, 0, 1, 3).reshape(n, outer * INNER * w)


def gather_scatter_return(x, cols, y, o, i):
    outer = lax.axis_size("seq") // INNER
    m, n, w = x.shape
    parts = cols.reshape(n, outer, INNER, w).transpose(2, 1, 0, 3)
    first = [jnp.concatenate([x, parts[i]])]
    for k in range(1, INNER):
        piece = lax.dynamic_index_in_dim(parts, (i + k) % INNER, 0, keepdims=False)
        first.append(lax.ppermute(jnp.concatenate([x, piece]), "seq", seq_pairs(k, 0)))
    first = jnp.stack(first, axis=1)
    own, rest = first[:m], first[m:]
    second = []
    back = [y[0]] + [None] * (outer - 1)
    for k in range(1, outer):
        piece = lax.dynamic_index_in_dim(rest, (o + k) % outer, 0, keepdims=False)
        payload = jnp.concatenate([own.reshape(m * INNER, n, w), piece, y[outer - k].astype(own.dtype)])
        got = lax.ppermute(payload, "seq", seq_pairs(k, 1))
        second.append(got[: (m + 1) * INNER])
        back[outer - k] = got[(m + 1) * INNER :]
    gathered = jnp.stack([own] + [s[: m * INNER].reshape(m, INNER, n, w) for s in second])
    scattered = jnp.stack([lax.dynamic_index_in_dim(rest, o, 0, keepdims=False)] + [s[m * INNER :] for s in second])
    back = jnp.stack(back, axis=1)
    returned = [back[0]]
    for k in range(1, INNER):
        returned.append(lax.ppermute(back[k], "seq", seq_pairs(INNER - k, 0)))
    returned = jnp.stack(returned, axis=1)
    returned = jnp.roll(jnp.roll(returned, o, axis=0), i, axis=1)
    return gathered, scattered, returned.transpose(2, 0, 1, 3).reshape(n, outer * INNER * w)


def contract_last(left, right):
    return lax.dot_general(
        left, right, (((1,), (1,)), ((), ())), preferred_element_type=jnp.float32
    )


def contract_first(left, right):
    return lax.dot_general(
        left, right, (((0,), (0,)), ((), ())), preferred_element_type=jnp.float32
    )


def normalize(values, gain):
    floats = values.astype(jnp.float32)
    inverse = lax.rsqrt(jnp.mean(floats * floats, axis=-1, keepdims=True) + 1e-05)
    unit = floats * inverse
    return (unit, inverse, unit * gain)


def per_device(
    up_activation,
    saved_projections,
    up_cotangent,
    up_input_weight,
    up_output_weight,
    upward_gain,
    accum_input,
    doc_starts,
):
    factor = HEAD ** (-0.5)
    width = GROUP * HEAD
    count = up_activation.shape[1]
    size = lax.axis_size("seq")
    outer = size // INNER
    me = lax.axis_index("seq")
    o, i = me // INNER, me % INNER
    first = me * count
    saved = saved_projections[0]
    cotangent = up_cotangent[0]
    unit_up, inverse_up, normed_up = normalize(up_activation[0], upward_gain[0])
    hidden = normed_up.astype(jnp.bfloat16)
    output_weight = lax.all_gather(up_output_weight[0], "seq", axis=1, tiled=True)
    key_value = gather_blocks(saved[:, width:]).reshape(size * count, 2 * HEAD)
    kv_weight_all = lax.all_gather(up_input_weight[0][:, width:], "seq", axis=0, tiled=True)
    keys = key_value[:, :HEAD]
    values = key_value[:, HEAD:]
    sources = (
        ((o - jnp.arange(outer, dtype=jnp.int32)) % outer)[:, None] * INNER
        + ((i - jnp.arange(INNER, dtype=jnp.int32)) % INNER)[None, :]
    ).reshape(size)
    key_positions = (sources[:, None] * count + jnp.arange(count, dtype=jnp.int32)[None, :]).reshape(-1)
    query = saved[:, :width].reshape(count, GROUP, HEAD)
    attn_grad = contract_last(cotangent, output_weight).astype(jnp.bfloat16)
    positions = first + jnp.arange(count, dtype=jnp.int32)
    starts = doc_starts[0]
    visible = (key_positions[None, :] <= positions[:, None]) & (
        key_positions[None, :] >= starts[:, None]
    )
    scores = jnp.einsum("tgh,jh->tgj", query, keys, preferred_element_type=jnp.float32) * factor
    scores = jnp.where(visible[:, None, :], scores, -1e30)
    top = jnp.max(scores, axis=-1, keepdims=True)
    exps = jnp.where(visible[:, None, :], jnp.exp(scores - top), 0.0)
    probs = exps / jnp.sum(exps, axis=-1, keepdims=True)
    weights = probs.astype(jnp.bfloat16)
    grad_heads = attn_grad.reshape(count, GROUP, HEAD)
    prob_grad = jnp.einsum("tgh,jh->tgj", grad_heads, values, preferred_element_type=jnp.float32)
    inner = jnp.sum(probs * prob_grad, axis=-1, keepdims=True)
    score_grad = (probs * (prob_grad - inner) * factor).astype(jnp.bfloat16)
    query_grad = (
        jnp.einsum("tgj,jh->tgh", score_grad, keys, preferred_element_type=jnp.float32)
        .astype(jnp.bfloat16)
        .reshape(count, width)
    )
    key_part = jnp.einsum("tgj,tgh->jh", score_grad, query, preferred_element_type=jnp.float32)
    value_part = jnp.einsum("tgj,tgh->jh", weights, grad_heads, preferred_element_type=jnp.float32)
    kv_part = jnp.concatenate([key_part, value_part], axis=1).reshape(outer, INNER, count, 2 * HEAD)
    query_all = gather_blocks(query_grad)
    kv_grad = reduce_blocks(kv_part, jnp.bfloat16).astype(jnp.bfloat16)
    block = contract_last(query_all.reshape(size * count, -1), up_input_weight[0][:, :width])
    kv_all, hidden_cols, hidden_grad = gather_scatter_return(
        kv_grad[None], hidden, block.astype(jnp.bfloat16).reshape(outer, INNER, count, -1), o, i
    )
    hidden_cols = hidden_cols.reshape(size * count, -1)
    grad_all = jnp.concatenate([query_all, kv_all[:, 0]], axis=-1).reshape(size * count, -1)
    input_term = contract_first(hidden_cols, grad_all).astype(jnp.bfloat16)
    hidden_grad = hidden_grad.astype(jnp.float32) + contract_last(kv_grad, kv_weight_all)
    scaled = hidden_grad * upward_gain[0]
    input_grad = cotangent.astype(jnp.float32) + inverse_up * (
        scaled - unit_up * jnp.mean(scaled * unit_up, axis=-1, keepdims=True)
    )
    moved_grad = shifted(input_grad.astype(jnp.bfloat16), "section", 1)
    mirror_input = mirrored(input_term, "section")
    project_grads = (accum_input[0].astype(jnp.float32) + mirror_input.astype(jnp.float32)).astype(
        jnp.bfloat16
    )
    return (moved_grad[None], project_grads[None])


def solution(mesh):
    return jax.shard_map(
        per_device,
        mesh=mesh,
        in_specs=(
            P("section", "seq", None),
            P("section", "seq", None),
            P("section", "seq", None),
            P("section", "seq", None),
            P("section", None, "seq"),
            P("section", None),
            P("section", "seq", None),
            P("section", "seq"),
        ),
        out_specs=(P("section", "seq", None), P("section", "seq", None)),
        check_vma=False,
    )
```

```python
import jax
import jax.numpy as jnp
from jax import lax
from jax.sharding import PartitionSpec as P

HEAD = 128
GROUP = 4
INNER = 4


def shifted(value, axis, steps):
    count = lax.axis_size(axis)
    initial, last = (max(0, -steps), min(count, count - steps))
    return lax.ppermute(value, axis, [(source, source + steps) for source in range(initial, last)])


def mirrored(value, axis):
    count = lax.axis_size(axis)
    return lax.ppermute(value, axis, [(source, count - 1 - source) for source in range(count)])


def seq_pairs(shift, level):
    size = lax.axis_size("seq")
    outer = size // INNER
    if level == 0:
        return [(o * INNER + i, o * INNER + (i + shift) % INNER) for o in range(outer) for i in range(INNER)]
    return [(o * INNER + i, ((o + shift) % outer) * INNER + i) for o in range(outer) for i in range(INNER)]


def gather_blocks(x):
    outer = lax.axis_size("seq") // INNER
    first = jnp.stack([x] + [lax.ppermute(x, "seq", seq_pairs(k, 0)) for k in range(1, INNER)])
    return jnp.stack([first] + [lax.ppermute(first, "seq", seq_pairs(k, 1)) for k in range(1, outer)])


def reduce_blocks(y, wire):
    outer = lax.axis_size("seq") // INNER
    acc = y[0]
    for k in range(1, outer):
        acc = acc + lax.ppermute(y[k].astype(wire), "seq", seq_pairs(outer - k, 1)).astype(y.dtype)
    total = acc[0]
    for k in range(1, INNER):
        total = total + lax.ppermute(acc[k].astype(wire), "seq", seq_pairs(INNER - k, 0)).astype(y.dtype)
    return total


def gather_and_scatter(x, cols, o, i):
    outer = lax.axis_size("seq") // INNER
    m, n, w = x.shape
    parts = cols.reshape(n, outer, INNER, w).transpose(2, 1, 0, 3)
    first = [jnp.concatenate([x, parts[i]])]
    for k in range(1, INNER):
        piece = lax.dynamic_index_in_dim(parts, (i + k) % INNER, 0, keepdims=False)
        first.append(lax.ppermute(jnp.concatenate([x, piece]), "seq", seq_pairs(k, 0)))
    first = jnp.stack(first, axis=1)
    own, rest = first[:m], first[m:]
    second = []
    for k in range(1, outer):
        piece = lax.dynamic_index_in_dim(rest, (o + k) % outer, 0, keepdims=False)
        payload = jnp.concatenate([own.reshape(m * INNER, n, w), piece])
        second.append(lax.ppermute(payload, "seq", seq_pairs(k, 1)))
    gathered = jnp.stack([own] + [s[: m * INNER].reshape(m, INNER, n, w) for s in second])
    scattered = jnp.stack([lax.dynamic_index_in_dim(rest, o, 0, keepdims=False)] + [s[m * INNER :] for s in second])
    return gathered, scattered


def gather_columns(y, o, i):
    outer = lax.axis_size("seq") // INNER
    n, w = y.shape[2], y.shape[3]
    first = [y[0]]
    for k in range(1, outer):
        first.append(lax.ppermute(y[k], "seq", seq_pairs(outer - k, 1)))
    first = jnp.stack(first, axis=1)
    second = [first[0]]
    for k in range(1, INNER):
        second.append(lax.ppermute(first[k], "seq", seq_pairs(INNER - k, 0)))
    second = jnp.stack(second, axis=1)
    second = jnp.roll(jnp.roll(second, o, axis=0), i, axis=1)
    return second.transpose(2, 0, 1, 3).reshape(n, outer * INNER * w)


def contract_last(left, right):
    return lax.dot_general(
        left, right, (((1,), (1,)), ((), ())), preferred_element_type=jnp.float32
    )


def contract_first(left, right):
    return lax.dot_general(
        left, right, (((0,), (0,)), ((), ())), preferred_element_type=jnp.float32
    )


def normalize(values, gain):
    floats = values.astype(jnp.float32)
    inverse = lax.rsqrt(jnp.mean(floats * floats, axis=-1, keepdims=True) + 1e-05)
    unit = floats * inverse
    return (unit, inverse, unit * gain)


def per_device(
    up_activation,
    saved_projections,
    up_cotangent,
    up_input_weight,
    up_output_weight,
    upward_gain,
    accum_input,
    doc_starts,
):
    factor = HEAD ** (-0.5)
    width = GROUP * HEAD
    count = up_activation.shape[1]
    size = lax.axis_size("seq")
    outer = size // INNER
    me = lax.axis_index("seq")
    o, i = me // INNER, me % INNER
    first = me * count
    saved = saved_projections[0]
    cotangent = up_cotangent[0]
    unit_up, inverse_up, normed_up = normalize(up_activation[0], upward_gain[0])
    hidden = normed_up.astype(jnp.bfloat16)
    output_weight = lax.all_gather(up_output_weight[0], "seq", axis=1, tiled=True)
    key_value = gather_blocks(saved[:, width:]).reshape(size * count, 2 * HEAD)
    kv_weight_all = lax.all_gather(up_input_weight[0][:, width:], "seq", axis=0, tiled=True)
    keys = key_value[:, :HEAD]
    values = key_value[:, HEAD:]
    sources = (
        ((o - jnp.arange(outer, dtype=jnp.int32)) % outer)[:, None] * INNER
        + ((i - jnp.arange(INNER, dtype=jnp.int32)) % INNER)[None, :]
    ).reshape(size)
    key_positions = (sources[:, None] * count + jnp.arange(count, dtype=jnp.int32)[None, :]).reshape(-1)
    query = saved[:, :width].reshape(count, GROUP, HEAD)
    positions = first + jnp.arange(count, dtype=jnp.int32)
    starts = doc_starts[0]
    visible = (key_positions[None, :] <= positions[:, None]) & (
        key_positions[None, :] >= starts[:, None]
    )
    scores = jnp.einsum("tgh,jh->tgj", query, keys, preferred_element_type=jnp.float32) * factor
    scores = jnp.where(visible[:, None, :], scores, -1e30)
    top = jnp.max(scores, axis=-1, keepdims=True)
    exps = jnp.where(visible[:, None, :], jnp.exp(scores - top), 0.0)
    probs = exps / jnp.sum(exps, axis=-1, keepdims=True)
    weights = probs.astype(jnp.bfloat16)
    probs, weights, output_weight = lax.optimization_barrier((probs, weights, output_weight))
    attn_grad = contract_last(cotangent, output_weight).astype(jnp.bfloat16)
    grad_heads = attn_grad.reshape(count, GROUP, HEAD)
    prob_grad = jnp.einsum("tgh,jh->tgj", grad_heads, values, preferred_element_type=jnp.float32)
    inner = jnp.sum(probs * prob_grad, axis=-1, keepdims=True)
    score_grad = (probs * (prob_grad - inner) * factor).astype(jnp.bfloat16)
    query_grad = (
        jnp.einsum("tgj,jh->tgh", score_grad, keys, preferred_element_type=jnp.float32)
        .astype(jnp.bfloat16)
        .reshape(count, width)
    )
    key_part = jnp.einsum("tgj,tgh->jh", score_grad, query, preferred_element_type=jnp.float32)
    value_part = jnp.einsum("tgj,tgh->jh", weights, grad_heads, preferred_element_type=jnp.float32)
    kv_part = jnp.concatenate([key_part, value_part], axis=1).reshape(outer, INNER, count, 2 * HEAD)
    query_all = gather_blocks(query_grad)
    kv_grad = reduce_blocks(kv_part, jnp.bfloat16).astype(jnp.bfloat16)
    kv_all, hidden_cols = gather_and_scatter(kv_grad[None], hidden, o, i)
    hidden_cols = hidden_cols.reshape(size * count, -1)
    grad_all = jnp.concatenate([query_all, kv_all[:, 0]], axis=-1).reshape(size * count, -1)
    input_term = contract_first(hidden_cols, grad_all).astype(jnp.bfloat16)
    block = contract_last(query_all.reshape(size * count, -1), up_input_weight[0][:, :width])
    hidden_grad = gather_columns(block.astype(jnp.bfloat16).reshape(outer, INNER, count, -1), o, i)
    hidden_grad = hidden_grad.astype(jnp.float32) + contract_last(kv_grad, kv_weight_all)
    scaled = hidden_grad * upward_gain[0]
    input_grad = cotangent.astype(jnp.float32) + inverse_up * (
        scaled - unit_up * jnp.mean(scaled * unit_up, axis=-1, keepdims=True)
    )
    moved_grad = shifted(input_grad.astype(jnp.bfloat16), "section", 1)
    mirror_input = mirrored(input_term, "section")
    project_grads = (accum_input[0].astype(jnp.float32) + mirror_input.astype(jnp.float32)).astype(
        jnp.bfloat16
    )
    return (moved_grad[None], project_grads[None])


def solution(mesh):
    return jax.shard_map(
        per_device,
        mesh=mesh,
        in_specs=(
            P("section", "seq", None),
            P("section", "seq", None),
            P("section", "seq", None),
            P("section", "seq", None),
            P("section", None, "seq"),
            P("section", None),
            P("section", "seq", None),
            P("section", "seq"),
        ),
        out_specs=(P("section", "seq", None), P("section", "seq", None)),
        check_vma=False,
    )
```

```python
import jax
import jax.numpy as jnp
from jax import lax
from jax.sharding import PartitionSpec as P

HEAD = 128
GROUP = 4
INNER = 4


def shifted(value, axis, steps):
    count = lax.axis_size(axis)
    initial, last = (max(0, -steps), min(count, count - steps))
    return lax.ppermute(value, axis, [(source, source + steps) for source in range(initial, last)])


def mirrored(value, axis):
    count = lax.axis_size(axis)
    return lax.ppermute(value, axis, [(source, count - 1 - source) for source in range(count)])


def seq_pairs(shift, level):
    size = lax.axis_size("seq")
    outer = size // INNER
    if level == 0:
        return [(o * INNER + i, o * INNER + (i + shift) % INNER) for o in range(outer) for i in range(INNER)]
    return [(o * INNER + i, ((o + shift) % outer) * INNER + i) for o in range(outer) for i in range(INNER)]


def gather_blocks(x):
    outer = lax.axis_size("seq") // INNER
    first = jnp.stack([x] + [lax.ppermute(x, "seq", seq_pairs(k, 0)) for k in range(1, INNER)])
    return jnp.stack([first] + [lax.ppermute(first, "seq", seq_pairs(k, 1)) for k in range(1, outer)])


def reduce_blocks(y, wire):
    outer = lax.axis_size("seq") // INNER
    acc = y[0]
    for k in range(1, outer):
        acc = acc + lax.ppermute(y[k].astype(wire), "seq", seq_pairs(outer - k, 1)).astype(y.dtype)
    total = acc[0]
    for k in range(1, INNER):
        total = total + lax.ppermute(acc[k].astype(wire), "seq", seq_pairs(INNER - k, 0)).astype(y.dtype)
    return total


def gather_and_scatter(x, cols, o, i):
    outer = lax.axis_size("seq") // INNER
    m, n, w = x.shape
    parts = cols.reshape(n, outer, INNER, w).transpose(2, 1, 0, 3)
    first = [jnp.concatenate([x, parts[i]])]
    for k in range(1, INNER):
        piece = lax.dynamic_index_in_dim(parts, (i + k) % INNER, 0, keepdims=False)
        first.append(lax.ppermute(jnp.concatenate([x, piece]), "seq", seq_pairs(k, 0)))
    first = jnp.stack(first, axis=1)
    own, rest = first[:m], first[m:]
    second = []
    for k in range(1, outer):
        piece = lax.dynamic_index_in_dim(rest, (o + k) % outer, 0, keepdims=False)
        payload = jnp.concatenate([own.reshape(m * INNER, n, w), piece])
        second.append(lax.ppermute(payload, "seq", seq_pairs(k, 1)))
    gathered = jnp.stack([own] + [s[: m * INNER].reshape(m, INNER, n, w) for s in second])
    scattered = jnp.stack([lax.dynamic_index_in_dim(rest, o, 0, keepdims=False)] + [s[m * INNER :] for s in second])
    return gathered, scattered


def gather_columns(y, o, i):
    outer = lax.axis_size("seq") // INNER
    n, w = y.shape[2], y.shape[3]
    first = [y[0]]
    for k in range(1, outer):
        first.append(lax.ppermute(y[k], "seq", seq_pairs(outer - k, 1)))
    first = jnp.stack(first, axis=1)
    second = [first[0]]
    for k in range(1, INNER):
        second.append(lax.ppermute(first[k], "seq", seq_pairs(INNER - k, 0)))
    second = jnp.stack(second, axis=1)
    second = jnp.roll(jnp.roll(second, o, axis=0), i, axis=1)
    return second.transpose(2, 0, 1, 3).reshape(n, outer * INNER * w)


def contract_last(left, right):
    return lax.dot_general(
        left, right, (((1,), (1,)), ((), ())), preferred_element_type=jnp.float32
    )


def contract_first(left, right):
    return lax.dot_general(
        left, right, (((0,), (0,)), ((), ())), preferred_element_type=jnp.float32
    )


def normalize(values, gain):
    floats = values.astype(jnp.float32)
    inverse = lax.rsqrt(jnp.mean(floats * floats, axis=-1, keepdims=True) + 1e-05)
    unit = floats * inverse
    return (unit, inverse, unit * gain)


def per_device(
    up_activation,
    saved_projections,
    up_cotangent,
    up_input_weight,
    up_output_weight,
    upward_gain,
    accum_input,
    doc_starts,
):
    factor = HEAD ** (-0.5)
    width = GROUP * HEAD
    count = up_activation.shape[1]
    size = lax.axis_size("seq")
    outer = size // INNER
    me = lax.axis_index("seq")
    o, i = me // INNER, me % INNER
    first = me * count
    saved = saved_projections[0]
    cotangent = up_cotangent[0]
    unit_up, inverse_up, normed_up = normalize(up_activation[0], upward_gain[0])
    hidden = normed_up.astype(jnp.bfloat16)
    output_weight = lax.all_gather(up_output_weight[0], "seq", axis=1, tiled=True)
    key_value = gather_blocks(saved[:, width:]).reshape(size * count, 2 * HEAD)
    kv_weight_all = lax.all_gather(up_input_weight[0][:, width:], "seq", axis=0, tiled=True)
    keys = key_value[:, :HEAD]
    values = key_value[:, HEAD:]
    sources = (
        ((o - jnp.arange(outer, dtype=jnp.int32)) % outer)[:, None] * INNER
        + ((i - jnp.arange(INNER, dtype=jnp.int32)) % INNER)[None, :]
    ).reshape(size)
    key_positions = (sources[:, None] * count + jnp.arange(count, dtype=jnp.int32)[None, :]).reshape(-1)
    query = saved[:, :width].reshape(count, GROUP, HEAD)
    attn_grad = contract_last(cotangent, output_weight).astype(jnp.bfloat16)
    positions = first + jnp.arange(count, dtype=jnp.int32)
    starts = doc_starts[0]
    visible = (key_positions[None, :] <= positions[:, None]) & (
        key_positions[None, :] >= starts[:, None]
    )
    scores = jnp.einsum("tgh,jh->tgj", query, keys, preferred_element_type=jnp.float32) * factor
    scores = jnp.where(visible[:, None, :], scores, -1e30)
    top = jnp.max(scores, axis=-1, keepdims=True)
    exps = jnp.where(visible[:, None, :], jnp.exp(scores - top), 0.0)
    probs = exps / jnp.sum(exps, axis=-1, keepdims=True)
    weights = probs.astype(jnp.bfloat16)
    grad_heads = attn_grad.reshape(count, GROUP, HEAD)
    prob_grad = jnp.einsum("tgh,jh->tgj", grad_heads, values, preferred_element_type=jnp.float32)
    inner = jnp.sum(probs * prob_grad, axis=-1, keepdims=True)
    score_grad = (probs * (prob_grad - inner) * factor).astype(jnp.bfloat16)
    query_grad = (
        jnp.einsum("tgj,jh->tgh", score_grad, keys, preferred_element_type=jnp.float32)
        .astype(jnp.bfloat16)
        .reshape(count, width)
    )
    key_part = jnp.einsum("tgj,tgh->jh", score_grad, query, preferred_element_type=jnp.float32)
    value_part = jnp.einsum("tgj,tgh->jh", weights, grad_heads, preferred_element_type=jnp.float32)
    kv_part = jnp.concatenate([key_part, value_part], axis=1).reshape(outer, INNER, count, 2 * HEAD)
    query_all = gather_blocks(query_grad)
    kv_grad = reduce_blocks(kv_part, jnp.float32).astype(jnp.bfloat16)
    kv_all, hidden_cols = gather_and_scatter(kv_grad[None], hidden, o, i)
    hidden_cols = hidden_cols.reshape(size * count, -1)
    grad_all = jnp.concatenate([query_all, kv_all[:, 0]], axis=-1).reshape(size * count, -1)
    input_term = contract_first(hidden_cols, grad_all).astype(jnp.bfloat16)
    block = contract_last(query_all.reshape(size * count, -1), up_input_weight[0][:, :width])
    hidden_grad = gather_columns(block.astype(jnp.bfloat16).reshape(outer, INNER, count, -1), o, i)
    hidden_grad = hidden_grad.astype(jnp.float32) + contract_last(kv_grad, kv_weight_all)
    scaled = hidden_grad * upward_gain[0]
    input_grad = cotangent.astype(jnp.float32) + inverse_up * (
        scaled - unit_up * jnp.mean(scaled * unit_up, axis=-1, keepdims=True)
    )
    moved_grad = shifted(input_grad.astype(jnp.bfloat16), "section", 1)
    mirror_input = mirrored(input_term, "section")
    project_grads = (accum_input[0].astype(jnp.float32) + mirror_input.astype(jnp.float32)).astype(
        jnp.bfloat16
    )
    return (moved_grad[None], project_grads[None])


def solution(mesh):
    return jax.shard_map(
        per_device,
        mesh=mesh,
        in_specs=(
            P("section", "seq", None),
            P("section", "seq", None),
            P("section", "seq", None),
            P("section", "seq", None),
            P("section", None, "seq"),
            P("section", None),
            P("section", "seq", None),
            P("section", "seq"),
        ),
        out_specs=(P("section", "seq", None), P("section", "seq", None)),
        check_vma=False,
    )
```

```python
import jax
import jax.numpy as jnp
from jax import lax
from jax.sharding import PartitionSpec as P

HEAD = 128
GROUP = 4
INNER = 4


def shifted(value, axis, steps):
    count = lax.axis_size(axis)
    initial, last = (max(0, -steps), min(count, count - steps))
    return lax.ppermute(value, axis, [(source, source + steps) for source in range(initial, last)])


def mirrored(value, axis):
    count = lax.axis_size(axis)
    return lax.ppermute(value, axis, [(source, count - 1 - source) for source in range(count)])


def seq_pairs(shift, level):
    size = lax.axis_size("seq")
    outer = size // INNER
    if level == 0:
        return [(o * INNER + i, o * INNER + (i + shift) % INNER) for o in range(outer) for i in range(INNER)]
    return [(o * INNER + i, ((o + shift) % outer) * INNER + i) for o in range(outer) for i in range(INNER)]


def gather_blocks(x):
    outer = lax.axis_size("seq") // INNER
    first = jnp.stack([x] + [lax.ppermute(x, "seq", seq_pairs(k, 0)) for k in range(1, INNER)])
    return jnp.stack([first] + [lax.ppermute(first, "seq", seq_pairs(k, 1)) for k in range(1, outer)])


def reduce_blocks(y, wire):
    outer = lax.axis_size("seq") // INNER
    acc = y[0]
    for k in range(1, outer):
        acc = acc + lax.ppermute(y[k].astype(wire), "seq", seq_pairs(outer - k, 1)).astype(y.dtype)
    total = acc[0]
    for k in range(1, INNER):
        total = total + lax.ppermute(acc[k].astype(wire), "seq", seq_pairs(INNER - k, 0)).astype(y.dtype)
    return total


def gather_and_scatter(x, cols, o, i):
    outer = lax.axis_size("seq") // INNER
    m, n, w = x.shape
    parts = cols.reshape(n, outer, INNER, w).transpose(2, 1, 0, 3)
    first = [jnp.concatenate([x, parts[i]])]
    for k in range(1, INNER):
        piece = lax.dynamic_index_in_dim(parts, (i + k) % INNER, 0, keepdims=False)
        first.append(lax.ppermute(jnp.concatenate([x, piece]), "seq", seq_pairs(k, 0)))
    first = jnp.stack(first, axis=1)
    own, rest = first[:m], first[m:]
    second = []
    for k in range(1, outer):
        piece = lax.dynamic_index_in_dim(rest, (o + k) % outer, 0, keepdims=False)
        payload = jnp.concatenate([own.reshape(m * INNER, n, w), piece])
        second.append(lax.ppermute(payload, "seq", seq_pairs(k, 1)))
    gathered = jnp.stack([own] + [s[: m * INNER].reshape(m, INNER, n, w) for s in second])
    scattered = jnp.stack([lax.dynamic_index_in_dim(rest, o, 0, keepdims=False)] + [s[m * INNER :] for s in second])
    return gathered, scattered


def gather_columns(y, o, i):
    outer = lax.axis_size("seq") // INNER
    n, w = y.shape[2], y.shape[3]
    first = [y[0]]
    for k in range(1, outer):
        first.append(lax.ppermute(y[k], "seq", seq_pairs(outer - k, 1)))
    first = jnp.stack(first, axis=1)
    second = [first[0]]
    for k in range(1, INNER):
        second.append(lax.ppermute(first[k], "seq", seq_pairs(INNER - k, 0)))
    second = jnp.stack(second, axis=1)
    second = jnp.roll(jnp.roll(second, o, axis=0), i, axis=1)
    return second.transpose(2, 0, 1, 3).reshape(n, outer * INNER * w)


def contract_last(left, right):
    return lax.dot_general(
        left, right, (((1,), (1,)), ((), ())), preferred_element_type=jnp.float32
    )


def contract_first(left, right):
    return lax.dot_general(
        left, right, (((0,), (0,)), ((), ())), preferred_element_type=jnp.float32
    )


def normalize(values, gain):
    floats = values.astype(jnp.float32)
    inverse = lax.rsqrt(jnp.mean(floats * floats, axis=-1, keepdims=True) + 1e-05)
    unit = floats * inverse
    return (unit, inverse, unit * gain)


def per_device(
    up_activation,
    saved_projections,
    up_cotangent,
    up_input_weight,
    up_output_weight,
    upward_gain,
    accum_input,
    doc_starts,
):
    factor = HEAD ** (-0.5)
    width = GROUP * HEAD
    count = up_activation.shape[1]
    size = lax.axis_size("seq")
    outer = size // INNER
    me = lax.axis_index("seq")
    o, i = me // INNER, me % INNER
    first = me * count
    saved = saved_projections[0]
    cotangent = up_cotangent[0]
    unit_up, inverse_up, normed_up = normalize(up_activation[0], upward_gain[0])
    hidden = normed_up.astype(jnp.bfloat16)
    output_weight = lax.all_gather(up_output_weight[0], "seq", axis=1, tiled=True)
    key_value, hidden_cols = gather_and_scatter(saved[None, :, width:], hidden, o, i)
    key_value = key_value[:, 0].reshape(size * count, 2 * HEAD)
    hidden_cols = hidden_cols.reshape(size * count, -1)
    kv_weight_all = lax.all_gather(up_input_weight[0][:, width:], "seq", axis=0, tiled=True)
    keys = key_value[:, :HEAD]
    values = key_value[:, HEAD:]
    sources = (
        ((o - jnp.arange(outer, dtype=jnp.int32)) % outer)[:, None] * INNER
        + ((i - jnp.arange(INNER, dtype=jnp.int32)) % INNER)[None, :]
    ).reshape(size)
    key_positions = (sources[:, None] * count + jnp.arange(count, dtype=jnp.int32)[None, :]).reshape(-1)
    query = saved[:, :width].reshape(count, GROUP, HEAD)
    attn_grad = contract_last(cotangent, output_weight).astype(jnp.bfloat16)
    positions = first + jnp.arange(count, dtype=jnp.int32)
    starts = doc_starts[0]
    visible = (key_positions[None, :] <= positions[:, None]) & (
        key_positions[None, :] >= starts[:, None]
    )
    scores = jnp.einsum("tgh,jh->tgj", query, keys, preferred_element_type=jnp.float32) * factor
    scores = jnp.where(visible[:, None, :], scores, -1e30)
    top = jnp.max(scores, axis=-1, keepdims=True)
    exps = jnp.where(visible[:, None, :], jnp.exp(scores - top), 0.0)
    probs = exps / jnp.sum(exps, axis=-1, keepdims=True)
    weights = probs.astype(jnp.bfloat16)
    grad_heads = attn_grad.reshape(count, GROUP, HEAD)
    prob_grad = jnp.einsum("tgh,jh->tgj", grad_heads, values, preferred_element_type=jnp.float32)
    inner = jnp.sum(probs * prob_grad, axis=-1, keepdims=True)
    score_grad = (probs * (prob_grad - inner) * factor).astype(jnp.bfloat16)
    query_grad = (
        jnp.einsum("tgj,jh->tgh", score_grad, keys, preferred_element_type=jnp.float32)
        .astype(jnp.bfloat16)
        .reshape(count, width)
    )
    key_part = jnp.einsum("tgj,tgh->jh", score_grad, query, preferred_element_type=jnp.float32)
    value_part = jnp.einsum("tgj,tgh->jh", weights, grad_heads, preferred_element_type=jnp.float32)
    kv_part = jnp.concatenate([key_part, value_part], axis=1).reshape(outer, INNER, count, 2 * HEAD)
    query_all = gather_blocks(query_grad)
    kv_grad = reduce_blocks(kv_part, jnp.bfloat16).astype(jnp.bfloat16)
    kv_all = gather_blocks(kv_grad)
    grad_all = jnp.concatenate([query_all, kv_all], axis=-1).reshape(size * count, -1)
    input_term = contract_first(hidden_cols, grad_all).astype(jnp.bfloat16)
    block = contract_last(query_all.reshape(size * count, -1), up_input_weight[0][:, :width])
    hidden_grad = gather_columns(block.astype(jnp.bfloat16).reshape(outer, INNER, count, -1), o, i)
    hidden_grad = hidden_grad.astype(jnp.float32) + contract_last(kv_grad, kv_weight_all)
    scaled = hidden_grad * upward_gain[0]
    input_grad = cotangent.astype(jnp.float32) + inverse_up * (
        scaled - unit_up * jnp.mean(scaled * unit_up, axis=-1, keepdims=True)
    )
    moved_grad = shifted(input_grad.astype(jnp.bfloat16), "section", 1)
    mirror_input = mirrored(input_term, "section")
    project_grads = (accum_input[0].astype(jnp.float32) + mirror_input.astype(jnp.float32)).astype(
        jnp.bfloat16
    )
    return (moved_grad[None], project_grads[None])


def solution(mesh):
    return jax.shard_map(
        per_device,
        mesh=mesh,
        in_specs=(
            P("section", "seq", None),
            P("section", "seq", None),
            P("section", "seq", None),
            P("section", "seq", None),
            P("section", None, "seq"),
            P("section", None),
            P("section", "seq", None),
            P("section", "seq"),
        ),
        out_specs=(P("section", "seq", None), P("section", "seq", None)),
        check_vma=False,
    )
```
